32 devices in a mesh: grp: 2 (over y), blk: 8 (over z, x), tch: 2 (over core).
Axes of the slice: x: 2, y: 2, z: 4, core: 2. Of those that a mesh axis runs over, the one named last changes fastest.
Arguments:
- samples: bfloat16 [4, 32, 65536], P('grp', 'blk', 'tch'), parts along dimension 0, may hold values from -6 to 6
- history: bfloat16 [4, 32, 15360], P('grp', 'blk'), parts along dimension 0, may hold values from -6 to 6
- coefficients: float32 [16, 1024], replicated, may hold values from -1.5 to 1.5
- station_of_slot: int32 [32], P('grp'), parts along dimension 0, may hold values from 0 to 15, each once
- station_ok: int32 [32], P('grp'), parts along dimension 0, may hold values from 0 to 1, as said below
Outputs:
- visibilities: bfloat16 [4, 1024, 32, 32], P('grp', ('blk', 'tch')), parts along dimension 0
The draws below stay inside these ranges and needn't reach their ends.
There are 2 independent parts, one for each index of `grp`. The reference program is written for one: setup_inputs(seed, part) draws one part's arguments, and reference() takes and returns one part's arrays. A program takes and returns all parts, laid end to end along the dimension named above; an argument that names none is the same for every part. Nothing has to cross between parts.
Inputs may be any that keep to these rules, and one draw needn't show every extreme that they name: `station_of_slot`: each station stands in exactly one slot. `station_ok`: 2 or 3 stations are flagged.
All inputs are finite; a program needn't handle non-finite values.
Results may differ from the reference program's by a relative error of at most 0.0074.
Values may be sent and summed in bfloat16 or wider, within the bound.
No kernel may reach another device: no remote copies, remote signals or barrier semaphores. Data moves between devices by JAX's collectives and lax.ppermute only.
A program may use at most 64 MiB of HBM per device.

```python
import math
import jax
import jax.numpy as jnp
from jax import lax

NFFT = 1024
TAPS = 16
STATIONS = 16
INPUTS = 32
NSPEC = 64


def draw_station_ok(key, part):
    flagged = STATIONS // 8 + part % 2
    order_vals = jax.random.permutation(jax.random.fold_in(key, 17), STATIONS).astype(jnp.int32)
    return (order_vals >= flagged).astype(jnp.int32)


def level_of(key, dims, split, low, high):
    gain = 1.0
    for dim, parts in split:
        steps = jax.random.uniform(jax.random.fold_in(jax.random.fold_in(key, 6), dim), (parts,), jnp.float32, low / len(split), high / len(split))
        gain = gain * jnp.repeat(jnp.exp(steps), dims[dim] // parts).reshape((-1,) + (1,) * (len(dims) - 1 - dim))
    return gain


def bell_draw(key, shape, width, bound, pieces=(), held_as=jnp.bfloat16):
    array = width * jax.random.normal(key, shape, jnp.float32)
    if pieces:
        array = array * level_of(key, shape, pieces, -0.22, 0.18)
    return jnp.clip(array, -bound, bound).astype(held_as)


def setup_inputs(seed: int = 0, part: int = 0) -> dict:
    key_of = jax.random.split(jax.random.key(seed), 6)
    part_splits = jax.random.split(jax.random.fold_in(key_of[5], part), 6)
    return {
        "samples": bell_draw(part_splits[0], (2, INPUTS, NSPEC * NFFT), 1.0, 6.0, ((1, 8), (2, 2))),
        "history": bell_draw(part_splits[1], (2, INPUTS, (TAPS - 1) * NFFT), 1.0, 6.0, ((1, 8),)),
        "coefficients": bell_draw(key_of[2], (TAPS, NFFT), TAPS ** -0.5, 1.5, (), jnp.float32),
        "station_of_slot": jax.random.permutation(part_splits[3], STATIONS).astype(jnp.int32),
        "station_ok": draw_station_ok(jax.random.fold_in(jax.random.fold_in(key_of[5], part), 71), part),
    }


def dft_table(fft_len):
    row_index = lax.broadcasted_iota(jnp.int32, (fft_len, fft_len), 0)
    col_index = lax.broadcasted_iota(jnp.int32, (fft_len, fft_len), 1)
    phase_step = row_index * col_index % fft_len
    angles = phase_step.astype(jnp.float32) * (2.0 * math.pi / fft_len)
    norm_scale = 1.0 / math.sqrt(fft_len)
    cosine = jnp.cos(angles) * norm_scale
    sine_part = jnp.sin(angles) * norm_scale
    upper_half = jnp.concatenate([cosine, -sine_part], axis=1)
    lower_half = jnp.concatenate([sine_part, cosine], axis=1)
    return jnp.concatenate([upper_half, lower_half], axis=0).astype(jnp.bfloat16)

def filter_bank(extended, coefficients, spec_count):
    tap_count, fft_len = coefficients.shape
    blocks = extended.reshape(extended.shape[0], extended.shape[1], -1, fft_len)
    running = jnp.zeros((extended.shape[0], extended.shape[1], spec_count, fft_len), jnp.float32)
    for tap_index in range(tap_count):
        running = running + coefficients[tap_index] * blocks[:, :, tap_index:tap_index + spec_count, :].astype(jnp.float32)
    return running.astype(jnp.bfloat16)

def channelize(filtered, dft_matrix):
    row_count, spec_count, fft_len = (filtered.shape[1], filtered.shape[2], filtered.shape[3])
    flat_rows = jnp.transpose(filtered, (1, 2, 0, 3)).reshape(row_count * spec_count, 2 * fft_len)
    product = jnp.dot(flat_rows, dft_matrix, preferred_element_type=jnp.float32).astype(jnp.bfloat16)
    return product.reshape(row_count, spec_count, 2, fft_len)

def reorder_inputs(values, station_of_slot, station_ok):
    station_count = station_of_slot.shape[0]
    input_count = values.shape[1]
    pol_count = input_count // station_count
    slot_index = jnp.zeros((station_count,), jnp.int32).at[station_of_slot].set(jnp.arange(station_count, dtype=jnp.int32))
    position = jnp.arange(input_count, dtype=jnp.int32)
    source_rows = (slot_index[position // pol_count] * pol_count + position % pol_count).astype(jnp.int32)
    keep_mask = station_ok[position // pol_count].astype(values.dtype)
    return jnp.take(values, source_rows, axis=1) * keep_mask[None, :, None]

def correlate(ordered, inverse_count):
    half_cols = ordered.shape[2] // 2
    rotated = jnp.concatenate([-ordered[:, :, half_cols:], ordered[:, :, :half_cols]], axis=2)
    real_vis = jnp.einsum('cak,cbk->cab', ordered, ordered)
    imag_vis = jnp.einsum('cak,cbk->cab', ordered, rotated)
    return (jnp.stack([real_vis, imag_vis], axis=0) * inverse_count).astype(jnp.bfloat16)

def reference(samples, history, coefficients, station_of_slot, station_ok):
    tap_count, fft_len = coefficients.shape
    spec_count = samples.shape[2] // fft_len
    extended = jnp.concatenate([history, samples], axis=2)
    filtered = filter_bank(extended, coefficients, spec_count)
    spectra = channelize(filtered, dft_table(fft_len))
    input_count = spectra.shape[0]
    channel_major = jnp.transpose(spectra, (3, 0, 2, 1)).reshape(fft_len, input_count, 2 * spec_count)
    ordered = reorder_inputs(channel_major, station_of_slot, station_ok)
    group_size = 8
    grouped = ordered.reshape(fft_len // group_size, group_size, input_count, 2 * spec_count)
    inverse_count = 1.0 / spec_count

    def correlate_group(group_values):
        return correlate(group_values.astype(jnp.float32), inverse_count)
    result = lax.map(correlate_group, grouped)
    return jnp.transpose(result, (1, 0, 2, 3, 4)).reshape(2, fft_len, input_count, input_count)
```

```python
import math

import numpy as np

import jax
import jax.numpy as jnp
from jax import lax
from jax.sharding import PartitionSpec as P

POLS = 2
RADIX = 4


def shifted(block, axis, distance):
    devices = range(lax.axis_size(axis))
    route = [(i - distance, i) for i in devices if i - distance in devices]
    return lax.ppermute(block, axis, route)


def dft_tables(fft_len):
    inner = fft_len // RADIX
    n2 = np.arange(inner)
    k1 = np.arange(RADIX)
    tw_angle = 2.0 * np.pi * np.outer(k1, n2) / fft_len
    twiddle_re = np.cos(tw_angle).astype(np.float32)
    twiddle_im = (-np.sin(tw_angle)).astype(np.float32)
    angle = 2.0 * np.pi * (np.outer(n2, n2) % inner) / inner
    scale = 1.0 / math.sqrt(fft_len)
    cosine = np.cos(angle) * scale
    sine_part = np.sin(angle) * scale
    upper_half = np.concatenate([cosine, -sine_part], axis=1)
    lower_half = np.concatenate([sine_part, cosine], axis=1)
    inner_matrix = np.concatenate([upper_half, lower_half], axis=0).astype(np.float32)
    return twiddle_re, twiddle_im, inner_matrix


def filter_bank(extended, coefficients, spec_count):
    tap_count, fft_len = coefficients.shape
    blocks = extended.reshape(extended.shape[0], extended.shape[1], -1, fft_len)
    running = jnp.zeros((extended.shape[0], extended.shape[1], spec_count, fft_len), jnp.float32)
    for tap_index in range(tap_count):
        running = running + coefficients[tap_index] * blocks[
            :, :, tap_index : tap_index + spec_count, :
        ].astype(jnp.float32)
    return running.astype(jnp.bfloat16)


def channelize(filtered):
    _, row_count, spec_count, fft_len = filtered.shape
    inner = fft_len // RADIX
    twiddle_re, twiddle_im, inner_matrix = dft_tables(fft_len)
    x = filtered.astype(jnp.float32).reshape(2, row_count, spec_count, RADIX, inner)
    xr = [x[0, :, :, j, :] for j in range(RADIX)]
    xi = [x[1, :, :, j, :] for j in range(RADIX)]
    ar, ai = xr[0] + xr[2], xi[0] + xi[2]
    br, bi = xr[1] + xr[3], xi[1] + xi[3]
    cr, ci = xr[0] - xr[2], xi[0] - xi[2]
    dr, di = xr[1] - xr[3], xi[1] - xi[3]
    yr = jnp.stack([ar + br, cr + di, ar - br, cr - di], axis=0)
    yi = jnp.stack([ai + bi, ci - dr, ai - bi, ci + dr], axis=0)
    tr = jnp.asarray(twiddle_re)[:, None, None, :]
    ti = jnp.asarray(twiddle_im)[:, None, None, :]
    zr = yr * tr - yi * ti
    zi = yr * ti + yi * tr
    z = jnp.concatenate([zr, zi], axis=-1)
    product = jnp.einsum(
        "kasn,nm->kasm",
        z,
        jnp.asarray(inner_matrix),
        precision=lax.Precision.HIGH,
        preferred_element_type=jnp.float32,
    ).astype(jnp.bfloat16)
    return product.reshape(RADIX, row_count, spec_count, 2, inner)


def reorder_inputs(values, station_of_slot, station_ok):
    station_count = station_of_slot.shape[0]
    input_count = values.shape[1]
    slot_index = (
        jnp.zeros((station_count,), jnp.int32)
        .at[station_of_slot]
        .set(jnp.arange(station_count, dtype=jnp.int32))
    )
    position = jnp.arange(input_count, dtype=jnp.int32)
    source_rows = slot_index[position // POLS] * POLS + position % POLS
    keep_mask = station_ok[position // POLS].astype(values.dtype)
    return jnp.take(values, source_rows, axis=1) * keep_mask[None, :, None]


def rotate_parts(ordered):
    half_cols = ordered.shape[2] // 2
    return jnp.concatenate([-ordered[:, :, half_cols:], ordered[:, :, :half_cols]], axis=2)


def correlate_full(ordered, inverse_count):
    rotated = rotate_parts(ordered)
    real_vis = jnp.einsum("cak,cbk->cab", ordered, ordered, preferred_element_type=jnp.float32)
    imag_vis = jnp.einsum("cak,cbk->cab", ordered, rotated, preferred_element_type=jnp.float32)
    return (jnp.stack([real_vis, imag_vis], axis=0) * inverse_count).astype(jnp.bfloat16)


def local(samples, history, coefficients, station_of_slot, station_ok):
    tap_count, fft_len = coefficients.shape
    row_count = samples.shape[1]
    spec_local = samples.shape[2] // fft_len
    half_count = lax.axis_size("tch")
    block_count = lax.axis_size("blk")
    dest_count = half_count * block_count
    spec_total = spec_local * half_count
    inner = fft_len // RADIX
    tail_block = jnp.concatenate([history, samples], axis=2)[:, :, -(tap_count - 1) * fft_len :]
    earlier = shifted(tail_block, "tch", 1)
    is_first = lax.axis_index("tch") == 0
    earlier = jnp.where(is_first, history, earlier)
    extended = jnp.concatenate([earlier, samples], axis=2)
    spectra = channelize(filter_bank(extended, coefficients, spec_local))
    kl_count = inner // dest_count
    spectra = spectra.reshape(RADIX, row_count, spec_local, 2, dest_count, kl_count)
    spectra = jnp.transpose(spectra, (4, 5, 0, 1, 3, 2))
    turned = lax.all_to_all(spectra, ("blk", "tch"), split_axis=0, concat_axis=0, tiled=True)
    layout = turned.reshape(block_count, half_count, kl_count, RADIX, row_count, 2, spec_local)
    layout = jnp.transpose(layout, (2, 3, 0, 4, 5, 1, 6))
    stacked = layout.reshape(kl_count * RADIX, block_count * row_count, 2 * spec_total)
    ordered = reorder_inputs(stacked, station_of_slot, station_ok)
    inverse_count = 1.0 / spec_total
    return correlate_full(ordered, inverse_count)


def solution(mesh):
    return jax.shard_map(
        local,
        mesh=mesh,
        in_specs=(P("grp", "blk", "tch"), P("grp", "blk", None), P(), P("grp"), P("grp")),
        out_specs=P("grp", ("blk", "tch"), None, None),
        check_vma=False,
    )
```

```python
import math

import numpy as np

import jax
import jax.numpy as jnp
from jax import lax
from jax.sharding import PartitionSpec as P

POLS = 2
RADIX = 4


def dft_tables(fft_len):
    inner = fft_len // RADIX
    n2 = np.arange(inner)
    k1 = np.arange(RADIX)
    tw_angle = 2.0 * np.pi * np.outer(k1, n2) / fft_len
    twiddle_re = np.cos(tw_angle).astype(np.float32)
    twiddle_im = (-np.sin(tw_angle)).astype(np.float32)
    angle = 2.0 * np.pi * (np.outer(n2, n2) % inner) / inner
    scale = 1.0 / math.sqrt(fft_len)
    inner_matrix = np.concatenate([np.cos(angle) * scale, np.sin(angle) * scale], axis=0)
    return twiddle_re, twiddle_im, inner_matrix.astype(np.float32)


def filter_bank(extended, coefficients, spec_count):
    tap_count, fft_len = coefficients.shape
    blocks = extended.reshape(extended.shape[0], extended.shape[1], -1, fft_len)
    running = jnp.zeros((extended.shape[0], extended.shape[1], spec_count, fft_len), jnp.float32)
    for tap_index in range(tap_count):
        running = running + coefficients[tap_index] * blocks[
            :, :, tap_index : tap_index + spec_count, :
        ].astype(jnp.float32)
    return running.astype(jnp.bfloat16)


def channelize(filtered):
    _, pol_count, spec_count, fft_len = filtered.shape
    inner = fft_len // RADIX
    twiddle_re, twiddle_im, inner_matrix = dft_tables(fft_len)
    x = filtered.astype(jnp.float32)
    xr = [x[0, :, :, j * inner : (j + 1) * inner] for j in range(RADIX)]
    xi = [x[1, :, :, j * inner : (j + 1) * inner] for j in range(RADIX)]
    ar, ai = xr[0] + xr[2], xi[0] + xi[2]
    br, bi = xr[1] + xr[3], xi[1] + xi[3]
    cr, ci = xr[0] - xr[2], xi[0] - xi[2]
    dr, di = xr[1] - xr[3], xi[1] - xi[3]
    yr = jnp.stack([ar + br, cr + di, ar - br, cr - di], axis=0)
    yi = jnp.stack([ai + bi, ci - dr, ai - bi, ci + dr], axis=0)
    tr = jnp.asarray(twiddle_re)[:, None, None, :]
    ti = jnp.asarray(twiddle_im)[:, None, None, :]
    zr = yr * tr - yi * ti
    zi = yr * ti + yi * tr
    real_rows = jnp.concatenate([zr, zi], axis=-1)
    imag_rows = jnp.concatenate([zi, -zr], axis=-1)
    rows = jnp.stack([real_rows, imag_rows], axis=2).reshape(RADIX * pol_count * 2 * spec_count, 2 * inner)
    product = lax.dot_general(
        jnp.asarray(inner_matrix),
        rows,
        (((0,), (1,)), ((), ())),
        precision=lax.Precision.HIGH,
        preferred_element_type=jnp.float32,
    )
    return product.astype(jnp.bfloat16)


def rotate_parts(ordered):
    half_cols = ordered.shape[2] // 2
    return jnp.concatenate([-ordered[:, :, half_cols:], ordered[:, :, :half_cols]], axis=2)


def correlate_full(ordered, inverse_count):
    rotated = rotate_parts(ordered)
    real_vis = jnp.einsum("cak,cbk->cab", ordered, ordered, preferred_element_type=jnp.float32)
    imag_vis = jnp.einsum("cak,cbk->cab", ordered, rotated, preferred_element_type=jnp.float32)
    return (jnp.stack([real_vis, imag_vis], axis=0) * inverse_count).astype(jnp.bfloat16)


def local(samples, history, coefficients, station_of_slot, station_ok):
    tap_count, fft_len = coefficients.shape
    row_count = samples.shape[1]
    half_count = lax.axis_size("tch")
    block_count = lax.axis_size("blk")
    dest_count = half_count * block_count
    station_count = station_of_slot.shape[0]
    inner = fft_len // RADIX
    kl_count = inner // dest_count
    keep = row_count // half_count
    t = lax.axis_index("tch")
    own = lax.dynamic_slice_in_dim(samples, t * keep, keep, axis=1)
    other = lax.dynamic_slice_in_dim(samples, (1 - t) * keep, keep, axis=1)
    received = lax.ppermute(other, "tch", [(0, 1), (1, 0)])
    is_first = t == 0
    first = jnp.where(is_first, own, received)
    second = jnp.where(is_first, received, own)
    earlier = lax.dynamic_slice_in_dim(history, t * keep, keep, axis=1)
    extended = jnp.concatenate([earlier, first, second], axis=2)
    spec_total = (extended.shape[2] - (tap_count - 1) * fft_len) // fft_len
    spectra = channelize(filter_bank(extended, coefficients, spec_total))
    spectra = spectra.reshape(dest_count, kl_count, -1)
    turned = lax.all_to_all(spectra, ("blk", "tch"), split_axis=0, concat_axis=0, tiled=True)
    slot_index = (
        jnp.zeros((station_count,), jnp.int32)
        .at[station_of_slot]
        .set(jnp.arange(station_count, dtype=jnp.int32))
    )
    keep_mask = station_ok.astype(turned.dtype)
    gathered = jnp.take(turned, slot_index, axis=0) * keep_mask[:, None, None]
    gathered = gathered.reshape(station_count, kl_count, RADIX, POLS, 2 * spec_total)
    ordered = jnp.transpose(gathered, (1, 2, 0, 3, 4)).reshape(
        kl_count * RADIX, station_count * POLS, 2 * spec_total
    )
    return correlate_full(ordered, 1.0 / spec_total)


def solution(mesh):
    return jax.shard_map(
        local,
        mesh=mesh,
        in_specs=(P("grp", "blk", "tch"), P("grp", "blk", None), P(), P("grp"), P("grp")),
        out_specs=P("grp", ("blk", "tch"), None, None),
        check_vma=False,
    )
```

```python
import math

import numpy as np

import jax
import jax.numpy as jnp
from jax import lax
from jax.sharding import PartitionSpec as P

POLS = 2
RADIX = 4


def dft_tables(fft_len):
    inner = fft_len // RADIX
    n2 = np.arange(inner)
    k1 = np.arange(RADIX)
    tw_angle = 2.0 * np.pi * np.outer(k1, n2) / fft_len
    twiddle_re = np.cos(tw_angle).astype(np.float32)
    twiddle_im = (-np.sin(tw_angle)).astype(np.float32)
    angle = 2.0 * np.pi * (np.outer(n2, n2) % inner) / inner
    scale = 1.0 / math.sqrt(fft_len)
    inner_matrix = np.concatenate([np.cos(angle) * scale, np.sin(angle) * scale], axis=0)
    return twiddle_re, twiddle_im, inner_matrix.astype(np.float32)


def filter_bank(extended, coefficients, spec_count):
    tap_count, fft_len = coefficients.shape
    blocks = extended.reshape(extended.shape[0], extended.shape[1], -1, fft_len)
    running = jnp.zeros((extended.shape[0], extended.shape[1], spec_count, fft_len), jnp.float32)
    for tap_index in range(tap_count):
        running = running + coefficients[tap_index] * blocks[
            :, :, tap_index : tap_index + spec_count, :
        ].astype(jnp.float32)
    return running.astype(jnp.bfloat16)


def channelize(filtered):
    _, pol_count, spec_count, fft_len = filtered.shape
    inner = fft_len // RADIX
    twiddle_re, twiddle_im, inner_matrix = dft_tables(fft_len)
    x = filtered.astype(jnp.float32)
    xr = [x[0, :, :, j * inner : (j + 1) * inner] for j in range(RADIX)]
    xi = [x[1, :, :, j * inner : (j + 1) * inner] for j in range(RADIX)]
    ar, ai = xr[0] + xr[2], xi[0] + xi[2]
    br, bi = xr[1] + xr[3], xi[1] + xi[3]
    cr, ci = xr[0] - xr[2], xi[0] - xi[2]
    dr, di = xr[1] - xr[3], xi[1] - xi[3]
    yr = jnp.stack([ar + br, cr + di, ar - br, cr - di], axis=0)
    yi = jnp.stack([ai + bi, ci - dr, ai - bi, ci + dr], axis=0)
    tr = jnp.asarray(twiddle_re)[:, None, None, :]
    ti = jnp.asarray(twiddle_im)[:, None, None, :]
    zr = yr * tr - yi * ti
    zi = yr * ti + yi * tr
    real_rows = jnp.concatenate([zr, zi], axis=-1)
    imag_rows = jnp.concatenate([zi, -zr], axis=-1)
    rows = jnp.stack([real_rows, imag_rows], axis=2).reshape(RADIX * pol_count * 2 * spec_count, 2 * inner)
    product = lax.dot_general(
        jnp.asarray(inner_matrix),
        rows,
        (((0,), (1,)), ((), ())),
        precision=lax.Precision.HIGH,
        preferred_element_type=jnp.float32,
    )
    return product.astype(jnp.bfloat16)


def rotate_parts(ordered):
    half_cols = ordered.shape[2] // 2
    return jnp.concatenate([-ordered[:, :, half_cols:], ordered[:, :, :half_cols]], axis=2)


def correlate_full(ordered, inverse_count):
    rotated = rotate_parts(ordered)
    real_vis = jnp.einsum("cak,cbk->cab", ordered, ordered, preferred_element_type=jnp.float32)
    imag_vis = jnp.einsum("cak,cbk->cab", ordered, rotated, preferred_element_type=jnp.float32)
    return (jnp.stack([real_vis, imag_vis], axis=0) * inverse_count).astype(jnp.bfloat16)


def local(samples, history, coefficients, station_of_slot, station_ok):
    tap_count, fft_len = coefficients.shape
    row_count = samples.shape[1]
    half_count = lax.axis_size("tch")
    block_count = lax.axis_size("blk")
    dest_count = half_count * block_count
    station_count = station_of_slot.shape[0]
    inner = fft_len // RADIX
    kl_count = inner // dest_count
    keep = row_count // half_count
    t = lax.axis_index("tch")
    own = lax.dynamic_slice_in_dim(samples, t * keep, keep, axis=1)
    other = lax.dynamic_slice_in_dim(samples, (1 - t) * keep, keep, axis=1)
    received = lax.ppermute(other, "tch", [(0, 1), (1, 0)])
    is_first = t == 0
    first = jnp.where(is_first, own, received)
    second = jnp.where(is_first, received, own)
    earlier = lax.dynamic_slice_in_dim(history, t * keep, keep, axis=1)
    extended = jnp.concatenate([earlier, first, second], axis=2)
    spec_total = (extended.shape[2] - (tap_count - 1) * fft_len) // fft_len
    slot_index = (
        jnp.zeros((station_count,), jnp.int32)
        .at[station_of_slot]
        .set(jnp.arange(station_count, dtype=jnp.int32))
    )
    keep_mask = station_ok.astype(jnp.bfloat16)
    by_pol = []
    pending = extended[:, 0:1]
    for pol in range(keep):
        spectra = channelize(filter_bank(pending, coefficients, spec_total))
        spectra = spectra.reshape(dest_count, kl_count, -1)
        if pol + 1 < keep:
            spectra, pending = lax.optimization_barrier((spectra, extended[:, pol + 1 : pol + 2]))
        turned = lax.all_to_all(spectra, ("blk", "tch"), split_axis=0, concat_axis=0, tiled=True)
        gathered = jnp.take(turned, slot_index, axis=0) * keep_mask[:, None, None]
        by_pol.append(gathered.reshape(station_count, kl_count, RADIX, 2 * spec_total))
    gathered = jnp.stack(by_pol, axis=1)
    ordered = jnp.transpose(gathered, (2, 3, 0, 1, 4)).reshape(
        kl_count * RADIX, station_count * keep, 2 * spec_total
    )
    return correlate_full(ordered, 1.0 / spec_total)


def solution(mesh):
    return jax.shard_map(
        local,
        mesh=mesh,
        in_specs=(P("grp", "blk", "tch"), P("grp", "blk", None), P(), P("grp"), P("grp")),
        out_specs=P("grp", ("blk", "tch"), None, None),
        check_vma=False,
    )
```

```python
import math

import numpy as np

import jax
import jax.numpy as jnp
from jax import lax
from jax.sharding import PartitionSpec as P

POLS = 2
RADIX = 4


def dft_tables(fft_len):
    inner = fft_len // RADIX
    n2 = np.arange(inner)
    k1 = np.arange(RADIX)
    tw_angle = 2.0 * np.pi * np.outer(k1, n2) / fft_len
    twiddle_re = np.cos(tw_angle).astype(np.float32)
    twiddle_im = (-np.sin(tw_angle)).astype(np.float32)
    angle = 2.0 * np.pi * (np.outer(n2, n2) % inner) / inner
    scale = 1.0 / math.sqrt(fft_len)
    inner_matrix = np.concatenate([np.cos(angle) * scale, np.sin(angle) * scale], axis=0)
    return twiddle_re, twiddle_im, inner_matrix.astype(np.float32)


def filter_bank(extended, coefficients, spec_count):
    tap_count, fft_len = coefficients.shape
    blocks = extended.reshape(extended.shape[0], extended.shape[1], -1, fft_len)
    weights = coefficients.reshape(tap_count, 1, fft_len)
    running = jnp.zeros((extended.shape[0], extended.shape[1], spec_count, fft_len), jnp.float32)
    for tap_index in range(tap_count):
        running = running + weights[tap_index] * blocks[
            :, :, tap_index : tap_index + spec_count, :
        ].astype(jnp.float32)
    return running.astype(jnp.bfloat16)


def channelize(filtered):
    _, pol_count, spec_count, fft_len = filtered.shape
    inner = fft_len // RADIX
    twiddle_re, twiddle_im, inner_matrix = dft_tables(fft_len)
    x = filtered.astype(jnp.float32)
    xr = [x[0, :, :, j * inner : (j + 1) * inner] for j in range(RADIX)]
    xi = [x[1, :, :, j * inner : (j + 1) * inner] for j in range(RADIX)]
    ar, ai = xr[0] + xr[2], xi[0] + xi[2]
    br, bi = xr[1] + xr[3], xi[1] + xi[3]
    cr, ci = xr[0] - xr[2], xi[0] - xi[2]
    dr, di = xr[1] - xr[3], xi[1] - xi[3]
    yr = jnp.stack([ar + br, cr + di, ar - br, cr - di], axis=0)
    yi = jnp.stack([ai + bi, ci - dr, ai - bi, ci + dr], axis=0)
    tr = jnp.asarray(twiddle_re)[:, None, None, :]
    ti = jnp.asarray(twiddle_im)[:, None, None, :]
    zr = yr * tr - yi * ti
    zi = yr * ti + yi * tr
    real_rows = jnp.concatenate([zr, zi], axis=-1)
    imag_rows = jnp.concatenate([zi, -zr], axis=-1)
    rows = jnp.stack([real_rows, imag_rows], axis=2).reshape(RADIX * pol_count * 2 * spec_count, 2 * inner)
    product = lax.dot_general(
        jnp.asarray(inner_matrix),
        rows,
        (((0,), (1,)), ((), ())),
        precision=lax.Precision.HIGH,
        preferred_element_type=jnp.float32,
    )
    return product.astype(jnp.bfloat16)


def rotate_parts(ordered):
    half_cols = ordered.shape[2] // 2
    return jnp.concatenate([-ordered[:, :, half_cols:], ordered[:, :, :half_cols]], axis=2)


def correlate_full(ordered, inverse_count):
    rotated = rotate_parts(ordered)
    real_vis = jnp.einsum("cak,cbk->cab", ordered, ordered, preferred_element_type=jnp.float32)
    imag_vis = jnp.einsum("cak,cbk->cab", ordered, rotated, preferred_element_type=jnp.float32)
    return (jnp.stack([real_vis, imag_vis], axis=0) * inverse_count).astype(jnp.bfloat16)


def local(samples, history, coefficients, station_of_slot, station_ok):
    tap_count, fft_len = coefficients.shape
    row_count = samples.shape[1]
    half_count = lax.axis_size("tch")
    block_count = lax.axis_size("blk")
    dest_count = half_count * block_count
    station_count = station_of_slot.shape[0]
    inner = fft_len // RADIX
    kl_count = inner // dest_count
    keep = row_count // half_count
    t = lax.axis_index("tch")
    blocks = samples.reshape(2, row_count, -1, fft_len)
    before = history.reshape(2, row_count, -1, fft_len)
    own = lax.dynamic_slice_in_dim(blocks, t * keep, keep, axis=1)
    other = lax.dynamic_slice_in_dim(blocks, (1 - t) * keep, keep, axis=1)
    received = lax.ppermute(other, "tch", [(0, 1), (1, 0)])
    is_first = t == 0
    first = jnp.where(is_first, own, received)
    second = jnp.where(is_first, received, own)
    earlier = lax.dynamic_slice_in_dim(before, t * keep, keep, axis=1)
    extended = jnp.concatenate([earlier, first, second], axis=2).reshape(2, keep, -1)
    spec_total = (extended.shape[2] - (tap_count - 1) * fft_len) // fft_len
    spectra = channelize(filter_bank(extended, coefficients, spec_total))
    spectra = spectra.reshape(dest_count, kl_count, -1)
    turned = lax.all_to_all(spectra, ("blk", "tch"), split_axis=0, concat_axis=0, tiled=True)
    slot_index = (
        jnp.zeros((station_count,), jnp.int32)
        .at[station_of_slot]
        .set(jnp.arange(station_count, dtype=jnp.int32))
    )
    keep_mask = station_ok.astype(turned.dtype)
    gathered = jnp.take(turned, slot_index, axis=0) * keep_mask[:, None, None]
    gathered = gathered.reshape(station_count, kl_count, RADIX, POLS, 2 * spec_total)
    ordered = jnp.transpose(gathered, (1, 2, 0, 3, 4)).reshape(
        kl_count * RADIX, station_count * POLS, 2 * spec_total
    )
    return correlate_full(ordered, 1.0 / spec_total)


def solution(mesh):
    return jax.shard_map(
        local,
        mesh=mesh,
        in_specs=(P("grp", "blk", "tch"), P("grp", "blk", None), P(), P("grp"), P("grp")),
        out_specs=P("grp", ("blk", "tch"), None, None),
        check_vma=False,
    )
```

```python
import math

import numpy as np

import jax
import jax.numpy as jnp
from jax import lax
from jax.sharding import PartitionSpec as P

POLS = 2
RADIX = 4


def dft_tables(fft_len):
    inner = fft_len // RADIX
    n2 = np.arange(inner)
    k1 = np.arange(RADIX)
    tw_angle = 2.0 * np.pi * np.outer(k1, n2) / fft_len
    twiddle_re = np.cos(tw_angle).astype(np.float32)
    twiddle_im = (-np.sin(tw_angle)).astype(np.float32)
    angle = 2.0 * np.pi * (np.outer(n2, n2) % inner) / inner
    scale = 1.0 / math.sqrt(fft_len)
    inner_matrix = np.concatenate([np.cos(angle) * scale, np.sin(angle) * scale], axis=0)
    return twiddle_re, twiddle_im, inner_matrix.astype(np.float32)


def filter_bank(extended, coefficients, spec_count):
    tap_count, fft_len = coefficients.shape
    blocks = extended.reshape(extended.shape[0], extended.shape[1], -1, fft_len)
    weights = coefficients.reshape(tap_count, 1, fft_len)
    running = jnp.zeros((extended.shape[0], extended.shape[1], spec_count, fft_len), jnp.float32)
    for tap_index in range(tap_count):
        running = running + weights[tap_index] * blocks[
            :, :, tap_index : tap_index + spec_count, :
        ].astype(jnp.float32)
    return running.astype(jnp.bfloat16)


def channelize(filtered):
    _, pol_count, spec_count, fft_len = filtered.shape
    inner = fft_len // RADIX
    twiddle_re, twiddle_im, inner_matrix = dft_tables(fft_len)
    x = filtered.astype(jnp.float32)
    xr = [x[0, :, :, j * inner : (j + 1) * inner] for j in range(RADIX)]
    xi = [x[1, :, :, j * inner : (j + 1) * inner] for j in range(RADIX)]
    ar, ai = xr[0] + xr[2], xi[0] + xi[2]
    br, bi = xr[1] + xr[3], xi[1] + xi[3]
    cr, ci = xr[0] - xr[2], xi[0] - xi[2]
    dr, di = xr[1] - xr[3], xi[1] - xi[3]
    yr = jnp.stack([ar + br, cr + di, ar - br, cr - di], axis=0)
    yi = jnp.stack([ai + bi, ci - dr, ai - bi, ci + dr], axis=0)
    tr = jnp.asarray(twiddle_re)[:, None, None, :]
    ti = jnp.asarray(twiddle_im)[:, None, None, :]
    zr = yr * tr - yi * ti
    zi = yr * ti + yi * tr
    real_rows = jnp.concatenate([zr, zi], axis=-1)
    imag_rows = jnp.concatenate([zi, -zr], axis=-1)
    rows = jnp.stack([real_rows, imag_rows], axis=2).reshape(RADIX * pol_count * 2 * spec_count, 2 * inner)
    rows_high = rows.astype(jnp.bfloat16)
    rows_rest = (rows - rows_high.astype(jnp.float32)).astype(jnp.bfloat16)
    table = inner_matrix.astype(jnp.bfloat16)
    product = lax.dot_general(
        jnp.concatenate([table, table], axis=0),
        jnp.concatenate([rows_high, rows_rest], axis=1),
        (((0,), (1,)), ((), ())),
        preferred_element_type=jnp.float32,
    )
    return product.astype(jnp.bfloat16)


def rotate_parts(ordered):
    half_cols = ordered.shape[2] // 2
    return jnp.concatenate([-ordered[:, :, half_cols:], ordered[:, :, :half_cols]], axis=2)


def correlate_full(ordered, inverse_count):
    both = jnp.concatenate([ordered, rotate_parts(ordered)], axis=1)
    vis = jnp.einsum("cak,cjk->caj", ordered, both, preferred_element_type=jnp.float32)
    input_count = ordered.shape[1]
    vis = jnp.stack([vis[:, :, :input_count], vis[:, :, input_count:]], axis=0)
    return (vis * inverse_count).astype(jnp.bfloat16)


def local(samples, history, coefficients, station_of_slot, station_ok):
    tap_count, fft_len = coefficients.shape
    row_count = samples.shape[1]
    half_count = lax.axis_size("tch")
    block_count = lax.axis_size("blk")
    dest_count = half_count * block_count
    station_count = station_of_slot.shape[0]
    inner = fft_len // RADIX
    kl_count = inner // dest_count
    keep = row_count // half_count
    t = lax.axis_index("tch")
    blocks = samples.reshape(2, row_count, -1, fft_len)
    before = history.reshape(2, row_count, -1, fft_len)
    own = lax.dynamic_slice_in_dim(blocks, t * keep, keep, axis=1)
    other = lax.dynamic_slice_in_dim(blocks, (1 - t) * keep, keep, axis=1)
    received = lax.ppermute(other, "tch", [(0, 1), (1, 0)])
    is_first = t == 0
    first = jnp.where(is_first, own, received)
    second = jnp.where(is_first, received, own)
    earlier = lax.dynamic_slice_in_dim(before, t * keep, keep, axis=1)
    extended = jnp.concatenate([earlier, first, second], axis=2).reshape(2, keep, -1)
    spec_total = (extended.shape[2] - (tap_count - 1) * fft_len) // fft_len
    spectra = channelize(filter_bank(extended, coefficients, spec_total))
    spectra = spectra.reshape(dest_count, kl_count, -1)
    turned = lax.all_to_all(spectra, ("blk", "tch"), split_axis=0, concat_axis=0, tiled=True)
    slot_index = (
        jnp.zeros((station_count,), jnp.int32)
        .at[station_of_slot]
        .set(jnp.arange(station_count, dtype=jnp.int32))
    )
    keep_mask = station_ok.astype(turned.dtype)
    gathered = jnp.take(turned, slot_index, axis=0) * keep_mask[:, None, None]
    gathered = gathered.reshape(station_count, kl_count, RADIX, POLS, 2 * spec_total)
    ordered = jnp.transpose(gathered, (1, 2, 0, 3, 4)).reshape(
        kl_count * RADIX, station_count * POLS, 2 * spec_total
    )
    return correlate_full(ordered, 1.0 / spec_total)


def solution(mesh):
    return jax.shard_map(
        local,
        mesh=mesh,
        in_specs=(P("grp", "blk", "tch"), P("grp", "blk", None), P(), P("grp"), P("grp")),
        out_specs=P("grp", ("blk", "tch"), None, None),
        check_vma=False,
    )
```

```python
import math

import numpy as np

import jax
import jax.numpy as jnp
from jax import lax
from jax.sharding import PartitionSpec as P

POLS = 2
RADIX = 4


def dft_tables(fft_len):
    inner = fft_len // RADIX
    n2 = np.arange(inner)
    k1 = np.arange(RADIX)
    tw_angle = 2.0 * np.pi * np.outer(k1, n2) / fft_len
    twiddle_re = np.cos(tw_angle).astype(np.float32)
    twiddle_im = (-np.sin(tw_angle)).astype(np.float32)
    angle = 2.0 * np.pi * (np.outer(n2, n2) % inner) / inner
    scale = 1.0 / math.sqrt(fft_len)
    inner_matrix = np.concatenate([np.cos(angle) * scale, np.sin(angle) * scale], axis=0)
    return twiddle_re, twiddle_im, inner_matrix.astype(np.float32)


def filter_bank(extended, coefficients, spec_count):
    tap_count, fft_len = coefficients.shape
    blocks = extended.reshape(extended.shape[0], extended.shape[1], -1, fft_len)
    weights = coefficients.reshape(tap_count, 1, fft_len)
    running = jnp.zeros((extended.shape[0], extended.shape[1], spec_count, fft_len), jnp.float32)
    for tap_index in range(tap_count):
        running = running + weights[tap_index] * blocks[
            :, :, tap_index : tap_index + spec_count, :
        ].astype(jnp.float32)
    return running.astype(jnp.bfloat16)


def channelize(filtered):
    _, pol_count, spec_count, fft_len = filtered.shape
    inner = fft_len // RADIX
    twiddle_re, twiddle_im, inner_matrix = dft_tables(fft_len)
    x = filtered.astype(jnp.float32)
    xr = [x[0, :, :, j * inner : (j + 1) * inner] for j in range(RADIX)]
    xi = [x[1, :, :, j * inner : (j + 1) * inner] for j in range(RADIX)]
    ar, ai = xr[0] + xr[2], xi[0] + xi[2]
    br, bi = xr[1] + xr[3], xi[1] + xi[3]
    cr, ci = xr[0] - xr[2], xi[0] - xi[2]
    dr, di = xr[1] - xr[3], xi[1] - xi[3]
    yr = jnp.stack([ar + br, cr + di, ar - br, cr - di], axis=0)
    yi = jnp.stack([ai + bi, ci - dr, ai - bi, ci + dr], axis=0)
    tr = jnp.asarray(twiddle_re)[:, None, None, :]
    ti = jnp.asarray(twiddle_im)[:, None, None, :]
    zr = yr * tr - yi * ti
    zi = yr * ti + yi * tr
    real_rows = jnp.concatenate([zr, zi], axis=-1)
    imag_rows = jnp.concatenate([zi, -zr], axis=-1)
    rows = jnp.stack([real_rows, imag_rows], axis=2).reshape(RADIX * pol_count * 2 * spec_count, 2 * inner)
    product = lax.dot_general(
        jnp.asarray(inner_matrix).astype(jnp.bfloat16),
        rows.astype(jnp.bfloat16),
        (((0,), (1,)), ((), ())),
        preferred_element_type=jnp.float32,
    )
    return product.astype(jnp.bfloat16)


def rotate_parts(ordered):
    half_cols = ordered.shape[2] // 2
    return jnp.concatenate([-ordered[:, :, half_cols:], ordered[:, :, :half_cols]], axis=2)


def correlate_full(ordered, inverse_count):
    rotated = rotate_parts(ordered)
    real_vis = jnp.einsum("cak,cbk->cab", ordered, ordered, preferred_element_type=jnp.float32)
    imag_vis = jnp.einsum("cak,cbk->cab", ordered, rotated, preferred_element_type=jnp.float32)
    return (jnp.stack([real_vis, imag_vis], axis=0) * inverse_count).astype(jnp.bfloat16)


def local(samples, history, coefficients, station_of_slot, station_ok):
    tap_count, fft_len = coefficients.shape
    row_count = samples.shape[1]
    half_count = lax.axis_size("tch")
    block_count = lax.axis_size("blk")
    dest_count = half_count * block_count
    station_count = station_of_slot.shape[0]
    inner = fft_len // RADIX
    kl_count = inner // dest_count
    keep = row_count // half_count
    t = lax.axis_index("tch")
    blocks = samples.reshape(2, row_count, -1, fft_len)
    before = history.reshape(2, row_count, -1, fft_len)
    own = lax.dynamic_slice_in_dim(blocks, t * keep, keep, axis=1)
    other = lax.dynamic_slice_in_dim(blocks, (1 - t) * keep, keep, axis=1)
    received = lax.ppermute(other, "tch", [(0, 1), (1, 0)])
    is_first = t == 0
    first = jnp.where(is_first, own, received)
    second = jnp.where(is_first, received, own)
    earlier = lax.dynamic_slice_in_dim(before, t * keep, keep, axis=1)
    extended = jnp.concatenate([earlier, first, second], axis=2).reshape(2, keep, -1)
    spec_total = (extended.shape[2] - (tap_count - 1) * fft_len) // fft_len
    spectra = channelize(filter_bank(extended, coefficients, spec_total))
    spectra = spectra.reshape(dest_count, kl_count, -1)
    turned = lax.all_to_all(spectra, ("blk", "tch"), split_axis=0, concat_axis=0, tiled=True)
    slot_index = (
        jnp.zeros((station_count,), jnp.int32)
        .at[station_of_slot]
        .set(jnp.arange(station_count, dtype=jnp.int32))
    )
    keep_mask = station_ok.astype(turned.dtype)
    gathered = jnp.take(turned, slot_index, axis=0) * keep_mask[:, None, None]
    gathered = gathered.reshape(station_count, kl_count, RADIX, POLS, 2 * spec_total)
    ordered = jnp.transpose(gathered, (1, 2, 0, 3, 4)).reshape(
        kl_count * RADIX, station_count * POLS, 2 * spec_total
    )
    return correlate_full(ordered, 1.0 / spec_total)


def solution(mesh):
    return jax.shard_map(
        local,
        mesh=mesh,
        in_specs=(P("grp", "blk", "tch"), P("grp", "blk", None), P(), P("grp"), P("grp")),
        out_specs=P("grp", ("blk", "tch"), None, None),
        check_vma=False,
    )
```

```python
import math

import numpy as np

import jax
import jax.numpy as jnp
from jax import lax
from jax.experimental.layout import Layout, with_layout_constraint
from jax.sharding import PartitionSpec as P

POLS = 2
RADIX = 4


def dft_tables(fft_len):
    inner = fft_len // RADIX
    n2 = np.arange(inner)
    k1 = np.arange(RADIX)
    tw_angle = 2.0 * np.pi * np.outer(k1, n2) / fft_len
    twiddle_re = np.cos(tw_angle).astype(np.float32)
    twiddle_im = (-np.sin(tw_angle)).astype(np.float32)
    angle = 2.0 * np.pi * (np.outer(n2, n2) % inner) / inner
    scale = 1.0 / math.sqrt(fft_len)
    inner_matrix = np.concatenate([np.cos(angle) * scale, np.sin(angle) * scale], axis=0)
    return twiddle_re, twiddle_im, inner_matrix.astype(np.float32)


def filter_bank(extended, coefficients, spec_count):
    tap_count, fft_len = coefficients.shape
    blocks = extended.reshape(extended.shape[0], extended.shape[1], -1, fft_len)
    weights = coefficients.reshape(tap_count, 1, fft_len)
    running = jnp.zeros((extended.shape[0], extended.shape[1], spec_count, fft_len), jnp.float32)
    for tap_index in range(tap_count):
        running = running + weights[tap_index] * blocks[
            :, :, tap_index : tap_index + spec_count, :
        ].astype(jnp.float32)
    return running.astype(jnp.bfloat16)


def channelize(filtered):
    _, pol_count, spec_count, fft_len = filtered.shape
    inner = fft_len // RADIX
    twiddle_re, twiddle_im, inner_matrix = dft_tables(fft_len)
    x = filtered.astype(jnp.float32)
    xr = [x[0, :, :, j * inner : (j + 1) * inner] for j in range(RADIX)]
    xi = [x[1, :, :, j * inner : (j + 1) * inner] for j in range(RADIX)]
    ar, ai = xr[0] + xr[2], xi[0] + xi[2]
    br, bi = xr[1] + xr[3], xi[1] + xi[3]
    cr, ci = xr[0] - xr[2], xi[0] - xi[2]
    dr, di = xr[1] - xr[3], xi[1] - xi[3]
    yr = jnp.stack([ar + br, cr + di, ar - br, cr - di], axis=0)
    yi = jnp.stack([ai + bi, ci - dr, ai - bi, ci + dr], axis=0)
    tr = jnp.asarray(twiddle_re)[:, None, None, :]
    ti = jnp.asarray(twiddle_im)[:, None, None, :]
    zr = yr * tr - yi * ti
    zi = yr * ti + yi * tr
    real_rows = jnp.concatenate([zr, zi], axis=-1)
    imag_rows = jnp.concatenate([zi, -zr], axis=-1)
    rows = jnp.stack([real_rows, imag_rows], axis=2).reshape(RADIX * pol_count * 2 * spec_count, 2 * inner)
    product = lax.dot_general(
        jnp.asarray(inner_matrix).astype(jnp.bfloat16),
        rows.astype(jnp.bfloat16),
        (((0,), (1,)), ((), ())),
        preferred_element_type=jnp.float32,
    )
    return product.astype(jnp.bfloat16)


def rotate_parts(ordered):
    half_cols = ordered.shape[2] // 2
    return jnp.concatenate([-ordered[:, :, half_cols:], ordered[:, :, :half_cols]], axis=2)


def correlate_full(ordered, inverse_count):
    rotated = rotate_parts(ordered)
    real_vis = jnp.einsum("cak,cbk->cab", ordered, ordered, preferred_element_type=jnp.float32)
    imag_vis = jnp.einsum("cak,cbk->cab", ordered, rotated, preferred_element_type=jnp.float32)
    return (jnp.stack([real_vis, imag_vis], axis=0) * inverse_count).astype(jnp.bfloat16)


def local(samples, history, coefficients, station_of_slot, station_ok):
    tap_count, fft_len = coefficients.shape
    row_count = samples.shape[1]
    half_count = lax.axis_size("tch")
    block_count = lax.axis_size("blk")
    dest_count = half_count * block_count
    station_count = station_of_slot.shape[0]
    inner = fft_len // RADIX
    kl_count = inner // dest_count
    keep = row_count // half_count
    t = lax.axis_index("tch")
    blocks = samples.reshape(2, row_count, -1, fft_len)
    before = history.reshape(2, row_count, -1, fft_len)
    own = lax.dynamic_slice_in_dim(blocks, t * keep, keep, axis=1)
    other = lax.dynamic_slice_in_dim(blocks, (1 - t) * keep, keep, axis=1)
    received = lax.ppermute(other, "tch", [(0, 1), (1, 0)])
    is_first = t == 0
    first = jnp.where(is_first, own, received)
    second = jnp.where(is_first, received, own)
    earlier = lax.dynamic_slice_in_dim(before, t * keep, keep, axis=1)
    extended = jnp.concatenate([earlier, first, second], axis=2).reshape(2, keep, -1)
    spec_total = (extended.shape[2] - (tap_count - 1) * fft_len) // fft_len
    spectra = channelize(filter_bank(extended, coefficients, spec_total))
    spectra = spectra.reshape(dest_count, kl_count, -1)
    turned = lax.all_to_all(spectra, ("blk", "tch"), split_axis=0, concat_axis=0, tiled=True)
    slot_index = (
        jnp.zeros((station_count,), jnp.int32)
        .at[station_of_slot]
        .set(jnp.arange(station_count, dtype=jnp.int32))
    )
    keep_mask = station_ok.astype(turned.dtype)
    gathered = jnp.take(turned, slot_index, axis=0) * keep_mask[:, None, None]
    gathered = gathered.reshape(station_count, kl_count, RADIX, POLS, 2 * spec_total)
    ordered = jnp.transpose(gathered, (1, 2, 0, 3, 4)).reshape(
        kl_count * RADIX, station_count * POLS, 2 * spec_total
    )
    vis = correlate_full(ordered, 1.0 / spec_total)
    return with_layout_constraint(vis, Layout((0, 1, 2, 3)))


def solution(mesh):
    return jax.shard_map(
        local,
        mesh=mesh,
        in_specs=(P("grp", "blk", "tch"), P("grp", "blk", None), P(), P("grp"), P("grp")),
        out_specs=P("grp", ("blk", "tch"), None, None),
        check_vma=False,
    )
```

```python
import math

import numpy as np

import jax
import jax.numpy as jnp
from jax import lax
from jax.experimental.layout import Layout, with_layout_constraint
from jax.sharding import PartitionSpec as P

POLS = 2
RADIX = 4


def dft_tables(fft_len):
    inner = fft_len // RADIX
    n2 = np.arange(inner)
    k1 = np.arange(RADIX)
    tw_angle = 2.0 * np.pi * np.outer(k1, n2) / fft_len
    twiddle_re = np.cos(tw_angle).astype(np.float32)
    twiddle_im = (-np.sin(tw_angle)).astype(np.float32)
    angle = 2.0 * np.pi * (np.outer(n2, n2) % inner) / inner
    scale = 1.0 / math.sqrt(fft_len)
    inner_matrix = np.concatenate([np.cos(angle) * scale, np.sin(angle) * scale], axis=0)
    return twiddle_re, twiddle_im, inner_matrix.astype(np.float32)


def filter_bank(extended, coefficients, spec_count):
    tap_count, fft_len = coefficients.shape
    blocks = extended.reshape(extended.shape[0], extended.shape[1], -1, fft_len)
    weights = coefficients.reshape(tap_count, 1, fft_len)
    running = jnp.zeros((extended.shape[0], extended.shape[1], spec_count, fft_len), jnp.float32)
    for tap_index in range(tap_count):
        running = running + weights[tap_index] * blocks[
            :, :, tap_index : tap_index + spec_count, :
        ].astype(jnp.float32)
    return running.astype(jnp.bfloat16)


def channelize(filtered):
    _, pol_count, spec_count, fft_len = filtered.shape
    inner = fft_len // RADIX
    twiddle_re, twiddle_im, inner_matrix = dft_tables(fft_len)
    x = filtered.astype(jnp.float32)
    xr = [x[0, :, :, j * inner : (j + 1) * inner] for j in range(RADIX)]
    xi = [x[1, :, :, j * inner : (j + 1) * inner] for j in range(RADIX)]
    ar, ai = xr[0] + xr[2], xi[0] + xi[2]
    br, bi = xr[1] + xr[3], xi[1] + xi[3]
    cr, ci = xr[0] - xr[2], xi[0] - xi[2]
    dr, di = xr[1] - xr[3], xi[1] - xi[3]
    yr = jnp.stack([ar + br, cr + di, ar - br, cr - di], axis=0)
    yi = jnp.stack([ai + bi, ci - dr, ai - bi, ci + dr], axis=0)
    tr = jnp.asarray(twiddle_re)[:, None, None, :]
    ti = jnp.asarray(twiddle_im)[:, None, None, :]
    zr = yr * tr - yi * ti
    zi = yr * ti + yi * tr
    real_rows = jnp.concatenate([zr, zi], axis=-1)
    imag_rows = jnp.concatenate([zi, -zr], axis=-1)
    rows = jnp.stack([real_rows, imag_rows], axis=2).reshape(RADIX * pol_count * 2 * spec_count, 2 * inner)
    product = lax.dot_general(
        jnp.asarray(inner_matrix).astype(jnp.bfloat16),
        rows.astype(jnp.bfloat16),
        (((0,), (1,)), ((), ())),
        preferred_element_type=jnp.float32,
    )
    return product.astype(jnp.bfloat16)


def rotate_parts(ordered):
    half_cols = ordered.shape[2] // 2
    return jnp.concatenate([-ordered[:, :, half_cols:], ordered[:, :, :half_cols]], axis=2)


def correlate_full(ordered, inverse_count):
    rotated = rotate_parts(ordered)
    real_vis = jnp.einsum("cak,cbk->cab", ordered, ordered, preferred_element_type=jnp.float32)
    imag_vis = jnp.einsum("cak,cbk->cab", ordered, rotated, preferred_element_type=jnp.float32)
    return (jnp.stack([real_vis, imag_vis], axis=0) * inverse_count).astype(jnp.bfloat16)


def local(samples, history, coefficients, station_of_slot, station_ok):
    tap_count, fft_len = coefficients.shape
    row_count = samples.shape[1]
    half_count = lax.axis_size("tch")
    block_count = lax.axis_size("blk")
    dest_count = half_count * block_count
    station_count = station_of_slot.shape[0]
    inner = fft_len // RADIX
    kl_count = inner // dest_count
    keep = row_count // half_count
    t = lax.axis_index("tch")
    other = lax.dynamic_slice_in_dim(samples, (1 - t) * keep, keep, axis=1).reshape(2, keep, -1, fft_len)
    received = lax.ppermute(other, "tch", [(0, 1), (1, 0)])
    own = lax.dynamic_slice_in_dim(samples, t * keep, keep, axis=1).reshape(2, keep, -1, fft_len)
    before = history.reshape(2, row_count, -1, fft_len)
    is_first = t == 0
    first = jnp.where(is_first, own, received)
    second = jnp.where(is_first, received, own)
    earlier = lax.dynamic_slice_in_dim(before, t * keep, keep, axis=1)
    extended = jnp.concatenate([earlier, first, second], axis=2).reshape(2, keep, -1)
    spec_total = (extended.shape[2] - (tap_count - 1) * fft_len) // fft_len
    spectra = channelize(filter_bank(extended, coefficients, spec_total))
    spectra = spectra.reshape(dest_count, kl_count, -1)
    turned = lax.all_to_all(spectra, ("blk", "tch"), split_axis=0, concat_axis=0, tiled=True)
    slot_index = (
        jnp.zeros((station_count,), jnp.int32)
        .at[station_of_slot]
        .set(jnp.arange(station_count, dtype=jnp.int32))
    )
    keep_mask = station_ok.astype(turned.dtype)
    gathered = jnp.take(turned, slot_index, axis=0) * keep_mask[:, None, None]
    gathered = gathered.reshape(station_count, kl_count, RADIX, POLS, 2 * spec_total)
    ordered = jnp.transpose(gathered, (1, 2, 0, 3, 4)).reshape(
        kl_count * RADIX, station_count * POLS, 2 * spec_total
    )
    vis = correlate_full(ordered, 1.0 / spec_total)
    return with_layout_constraint(vis, Layout((0, 1, 2, 3)))


def solution(mesh):
    return jax.shard_map(
        local,
        mesh=mesh,
        in_specs=(P("grp", "blk", "tch"), P("grp", "blk", None), P(), P("grp"), P("grp")),
        out_specs=P("grp", ("blk", "tch"), None, None),
        check_vma=False,
    )
```

```python
import math

import numpy as np

import jax
import jax.numpy as jnp
from jax import lax
from jax.experimental.layout import Layout, with_layout_constraint
from jax.sharding import PartitionSpec as P

POLS = 2
RADIX = 4


def dft_tables(fft_len):
    inner = fft_len // RADIX
    n2 = np.arange(inner)
    k1 = np.arange(RADIX)
    tw_angle = 2.0 * np.pi * np.outer(k1, n2) / fft_len
    twiddle_re = np.cos(tw_angle).astype(np.float32)
    twiddle_im = (-np.sin(tw_angle)).astype(np.float32)
    angle = 2.0 * np.pi * (np.outer(n2, n2) % inner) / inner
    scale = 1.0 / math.sqrt(fft_len)
    inner_matrix = np.concatenate([np.cos(angle) * scale, np.sin(angle) * scale], axis=0)
    return twiddle_re, twiddle_im, inner_matrix.astype(np.float32)


def filter_bank(extended, coefficients, spec_count):
    tap_count, fft_len = coefficients.shape
    blocks = extended.reshape(extended.shape[0], extended.shape[1], -1, fft_len)
    weights = coefficients.reshape(tap_count, 1, fft_len)
    running = jnp.zeros((extended.shape[0], extended.shape[1], spec_count, fft_len), jnp.float32)
    for tap_index in range(tap_count):
        running = running + weights[tap_index] * blocks[
            :, :, tap_index : tap_index + spec_count, :
        ].astype(jnp.float32)
    return running.astype(jnp.bfloat16)


def channelize(filtered):
    _, pol_count, spec_count, fft_len = filtered.shape
    inner = fft_len // RADIX
    twiddle_re, twiddle_im, inner_matrix = dft_tables(fft_len)
    x = filtered.astype(jnp.float32)
    xr = [x[0, :, :, j * inner : (j + 1) * inner] for j in range(RADIX)]
    xi = [x[1, :, :, j * inner : (j + 1) * inner] for j in range(RADIX)]
    ar, ai = xr[0] + xr[2], xi[0] + xi[2]
    br, bi = xr[1] + xr[3], xi[1] + xi[3]
    cr, ci = xr[0] - xr[2], xi[0] - xi[2]
    dr, di = xr[1] - xr[3], xi[1] - xi[3]
    yr = jnp.stack([ar + br, cr + di, ar - br, cr - di], axis=0)
    yi = jnp.stack([ai + bi, ci - dr, ai - bi, ci + dr], axis=0)
    tr = jnp.asarray(twiddle_re)[:, None, None, :]
    ti = jnp.asarray(twiddle_im)[:, None, None, :]
    zr = yr * tr - yi * ti
    zi = yr * ti + yi * tr
    real_rows = jnp.concatenate([zr, zi], axis=-1)
    imag_rows = jnp.concatenate([zi, -zr], axis=-1)
    rows = jnp.stack([real_rows, imag_rows], axis=2).reshape(RADIX * pol_count * 2 * spec_count, 2 * inner)
    product = lax.dot_general(
        jnp.asarray(inner_matrix).astype(jnp.bfloat16),
        rows.astype(jnp.bfloat16),
        (((0,), (1,)), ((), ())),
        preferred_element_type=jnp.float32,
    )
    return product.astype(jnp.bfloat16)


def rotate_parts(ordered):
    half_cols = ordered.shape[2] // 2
    return jnp.concatenate([-ordered[:, :, half_cols:], ordered[:, :, :half_cols]], axis=2)


def correlate_full(ordered, inverse_count):
    rotated = rotate_parts(ordered)
    real_vis = jnp.einsum("cak,cbk->cab", ordered, ordered, preferred_element_type=jnp.float32)
    imag_vis = jnp.einsum("cak,cbk->cab", ordered, rotated, preferred_element_type=jnp.float32)
    return (jnp.stack([real_vis, imag_vis], axis=0) * inverse_count).astype(jnp.bfloat16)


def local(samples, history, coefficients, station_of_slot, station_ok):
    tap_count, fft_len = coefficients.shape
    row_count = samples.shape[1]
    half_count = lax.axis_size("tch")
    block_count = lax.axis_size("blk")
    dest_count = half_count * block_count
    station_count = station_of_slot.shape[0]
    inner = fft_len // RADIX
    kl_count = inner // dest_count
    keep = row_count // half_count
    t = lax.axis_index("tch")
    blocks = samples.reshape(2, row_count, -1, fft_len)
    before = history.reshape(2, row_count, -1, fft_len)
    own = lax.dynamic_slice_in_dim(blocks, t * keep, keep, axis=1)
    other = lax.dynamic_slice_in_dim(blocks, (1 - t) * keep, keep, axis=1)
    received = lax.ppermute(other, "tch", [(0, 1), (1, 0)])
    is_first = t == 0
    first = jnp.where(is_first, own, received)
    second = jnp.where(is_first, received, own)
    earlier = lax.dynamic_slice_in_dim(before, t * keep, keep, axis=1)
    extended = jnp.concatenate([earlier, first, second], axis=2).astype(jnp.float32).reshape(2, keep, -1)
    spec_total = (extended.shape[2] - (tap_count - 1) * fft_len) // fft_len
    spectra = channelize(filter_bank(extended, coefficients, spec_total))
    spectra = spectra.reshape(dest_count, kl_count, -1)
    turned = lax.all_to_all(spectra, ("blk", "tch"), split_axis=0, concat_axis=0, tiled=True)
    slot_index = (
        jnp.zeros((station_count,), jnp.int32)
        .at[station_of_slot]
        .set(jnp.arange(station_count, dtype=jnp.int32))
    )
    keep_mask = station_ok.astype(turned.dtype)
    gathered = jnp.take(turned, slot_index, axis=0) * keep_mask[:, None, None]
    gathered = gathered.reshape(station_count, kl_count, RADIX, POLS, 2 * spec_total)
    ordered = jnp.transpose(gathered, (1, 2, 0, 3, 4)).reshape(
        kl_count * RADIX, station_count * POLS, 2 * spec_total
    )
    vis = correlate_full(ordered, 1.0 / spec_total)
    return with_layout_constraint(vis, Layout((0, 1, 2, 3)))


def solution(mesh):
    return jax.shard_map(
        local,
        mesh=mesh,
        in_specs=(P("grp", "blk", "tch"), P("grp", "blk", None), P(), P("grp"), P("grp")),
        out_specs=P("grp", ("blk", "tch"), None, None),
        check_vma=False,
    )
```

```python
import math

import numpy as np

import jax
import jax.numpy as jnp
from jax import lax
from jax.experimental.layout import Layout, with_layout_constraint
from jax.sharding import PartitionSpec as P

POLS = 2
RADIX = 4


def dft_tables(fft_len):
    inner = fft_len // RADIX
    n2 = np.arange(inner)
    k1 = np.arange(RADIX)
    tw_angle = 2.0 * np.pi * np.outer(k1, n2) / fft_len
    twiddle_re = np.cos(tw_angle).astype(np.float32)
    twiddle_im = (-np.sin(tw_angle)).astype(np.float32)
    angle = 2.0 * np.pi * (np.outer(n2, n2) % inner) / inner
    scale = 1.0 / math.sqrt(fft_len)
    inner_matrix = np.concatenate([np.cos(angle) * scale, np.sin(angle) * scale], axis=0)
    return twiddle_re, twiddle_im, inner_matrix.astype(np.float32)


def filter_bank(extended, coefficients, spec_count):
    tap_count, fft_len = coefficients.shape
    blocks = extended.reshape(extended.shape[0], extended.shape[1], -1, fft_len)
    weights = coefficients.reshape(tap_count, 1, fft_len)
    running = jnp.zeros((extended.shape[0], extended.shape[1], spec_count, fft_len), jnp.float32)
    for tap_index in range(tap_count):
        running = running + weights[tap_index] * blocks[
            :, :, tap_index : tap_index + spec_count, :
        ].astype(jnp.float32)
    return running.astype(jnp.bfloat16)


def channelize(filtered, origin):
    _, pol_count, spec_count, fft_len = filtered.shape
    inner = fft_len // RADIX
    twiddle_re, twiddle_im, inner_matrix = dft_tables(fft_len)
    x = filtered.astype(jnp.float32)
    xr = [x[0, :, :, j * inner : (j + 1) * inner] for j in range(RADIX)]
    xi = [x[1, :, :, j * inner : (j + 1) * inner] for j in range(RADIX)]
    ar, ai = xr[0] + xr[2], xi[0] + xi[2]
    br, bi = xr[1] + xr[3], xi[1] + xi[3]
    cr, ci = xr[0] - xr[2], xi[0] - xi[2]
    dr, di = xr[1] - xr[3], xi[1] - xi[3]
    yr = jnp.stack([ar + br, cr + di, ar - br, cr - di], axis=0)
    yi = jnp.stack([ai + bi, ci - dr, ai - bi, ci + dr], axis=0)
    angle = jnp.asarray(2.0 * np.pi * np.outer(np.arange(RADIX), np.arange(inner)) / fft_len, jnp.float32) + origin
    tr, ti, inner_matrix = lax.optimization_barrier(
        (jnp.cos(angle), -jnp.sin(angle), (jnp.asarray(inner_matrix) + origin).astype(jnp.bfloat16))
    )
    tr = tr[:, None, None, :]
    ti = ti[:, None, None, :]
    zr = yr * tr - yi * ti
    zi = yr * ti + yi * tr
    real_rows = jnp.concatenate([zr, zi], axis=-1)
    imag_rows = jnp.concatenate([zi, -zr], axis=-1)
    rows = jnp.stack([real_rows, imag_rows], axis=2).reshape(RADIX * pol_count * 2 * spec_count, 2 * inner)
    product = lax.dot_general(
        inner_matrix,
        rows.astype(jnp.bfloat16),
        (((0,), (1,)), ((), ())),
        preferred_element_type=jnp.float32,
    )
    return product.astype(jnp.bfloat16)


def rotate_parts(ordered):
    half_cols = ordered.shape[2] // 2
    return jnp.concatenate([-ordered[:, :, half_cols:], ordered[:, :, :half_cols]], axis=2)


def correlate_full(ordered, inverse_count):
    rotated = rotate_parts(ordered)
    real_vis = jnp.einsum("cak,cbk->cab", ordered, ordered, preferred_element_type=jnp.float32)
    imag_vis = jnp.einsum("cak,cbk->cab", ordered, rotated, preferred_element_type=jnp.float32)
    return (jnp.stack([real_vis, imag_vis], axis=0) * inverse_count).astype(jnp.bfloat16)


def local(samples, history, coefficients, station_of_slot, station_ok):
    tap_count, fft_len = coefficients.shape
    row_count = samples.shape[1]
    half_count = lax.axis_size("tch")
    block_count = lax.axis_size("blk")
    dest_count = half_count * block_count
    station_count = station_of_slot.shape[0]
    inner = fft_len // RADIX
    kl_count = inner // dest_count
    keep = row_count // half_count
    t = lax.axis_index("tch")
    blocks = samples.reshape(2, row_count, -1, fft_len)
    before = history.reshape(2, row_count, -1, fft_len)
    own = lax.dynamic_slice_in_dim(blocks, t * keep, keep, axis=1)
    other = lax.dynamic_slice_in_dim(blocks, (1 - t) * keep, keep, axis=1)
    received = lax.ppermute(other, "tch", [(0, 1), (1, 0)])
    is_first = t == 0
    first = jnp.where(is_first, own, received)
    second = jnp.where(is_first, received, own)
    earlier = lax.dynamic_slice_in_dim(before, t * keep, keep, axis=1)
    extended = jnp.concatenate([earlier, first, second], axis=2).reshape(2, keep, -1)
    spec_total = (extended.shape[2] - (tap_count - 1) * fft_len) // fft_len
    spectra = channelize(filter_bank(extended, coefficients, spec_total), 0.0 * coefficients[0, 0])
    spectra = spectra.reshape(dest_count, kl_count, -1)
    turned = lax.all_to_all(spectra, ("blk", "tch"), split_axis=0, concat_axis=0, tiled=True)
    slot_index = (
        jnp.zeros((station_count,), jnp.int32)
        .at[station_of_slot]
        .set(jnp.arange(station_count, dtype=jnp.int32))
    )
    keep_mask = station_ok.astype(turned.dtype)
    gathered = jnp.take(turned, slot_index, axis=0) * keep_mask[:, None, None]
    gathered = gathered.reshape(station_count, kl_count, RADIX, POLS, 2 * spec_total)
    ordered = jnp.transpose(gathered, (1, 2, 0, 3, 4)).reshape(
        kl_count * RADIX, station_count * POLS, 2 * spec_total
    )
    vis = correlate_full(ordered, 1.0 / spec_total)
    return with_layout_constraint(vis, Layout((0, 1, 2, 3)))


def solution(mesh):
    return jax.shard_map(
        local,
        mesh=mesh,
        in_specs=(P("grp", "blk", "tch"), P("grp", "blk", None), P(), P("grp"), P("grp")),
        out_specs=P("grp", ("blk", "tch"), None, None),
        check_vma=False,
    )
```

```python
import math

import numpy as np

import jax
import jax.numpy as jnp
from jax import lax
from jax.experimental.layout import Layout, with_layout_constraint
from jax.sharding import PartitionSpec as P

POLS = 2
RADIX = 4


def dft_tables(fft_len):
    inner = fft_len // RADIX
    n2 = np.arange(inner)
    k1 = np.arange(RADIX)
    tw_angle = 2.0 * np.pi * np.outer(k1, n2) / fft_len
    twiddle_re = np.cos(tw_angle).astype(np.float32)
    twiddle_im = (-np.sin(tw_angle)).astype(np.float32)
    angle = 2.0 * np.pi * (np.outer(n2, n2) % inner) / inner
    scale = 1.0 / math.sqrt(fft_len)
    inner_matrix = np.concatenate([np.cos(angle) * scale, np.sin(angle) * scale], axis=0)
    return twiddle_re, twiddle_im, inner_matrix.astype(np.float32)


def filter_bank(extended, coefficients, spec_count):
    tap_count, fft_len = coefficients.shape
    blocks = extended.reshape(extended.shape[0], extended.shape[1], -1, fft_len)
    weights = coefficients.reshape(tap_count, 1, fft_len)
    running = jnp.zeros((extended.shape[0], extended.shape[1], spec_count, fft_len), jnp.float32)
    for tap_index in range(tap_count):
        running = running + weights[tap_index] * blocks[
            :, :, tap_index : tap_index + spec_count, :
        ].astype(jnp.float32)
    return running.astype(jnp.bfloat16)


def channelize(filtered, origin):
    _, pol_count, spec_count, fft_len = filtered.shape
    inner = fft_len // RADIX
    twiddle_re, twiddle_im, inner_matrix = dft_tables(fft_len)
    x = filtered.astype(jnp.float32)
    xr = [x[0, :, :, j * inner : (j + 1) * inner] for j in range(RADIX)]
    xi = [x[1, :, :, j * inner : (j + 1) * inner] for j in range(RADIX)]
    ar, ai = xr[0] + xr[2], xi[0] + xi[2]
    br, bi = xr[1] + xr[3], xi[1] + xi[3]
    cr, ci = xr[0] - xr[2], xi[0] - xi[2]
    dr, di = xr[1] - xr[3], xi[1] - xi[3]
    yr = jnp.stack([ar + br, cr + di, ar - br, cr - di], axis=0)
    yi = jnp.stack([ai + bi, ci - dr, ai - bi, ci + dr], axis=0)
    angle = jnp.asarray(2.0 * np.pi * np.outer(np.arange(RADIX), np.arange(inner)) / fft_len, jnp.float32) + origin
    tr, ti, inner_matrix = lax.optimization_barrier(
        (jnp.cos(angle), -jnp.sin(angle), (jnp.asarray(inner_matrix) + origin).astype(jnp.bfloat16))
    )
    tr = tr[:, None, None, :]
    ti = ti[:, None, None, :]
    zr = yr * tr - yi * ti
    zi = yr * ti + yi * tr
    real_rows = jnp.concatenate([zr, zi], axis=-1)
    imag_rows = jnp.concatenate([zi, -zr], axis=-1)
    rows = jnp.stack([real_rows, imag_rows], axis=2).reshape(RADIX * pol_count * 2 * spec_count, 2 * inner)
    product = lax.dot_general(
        inner_matrix,
        rows.astype(jnp.bfloat16),
        (((0,), (1,)), ((), ())),
        preferred_element_type=jnp.float32,
    )
    return product.astype(jnp.bfloat16)


def rotate_parts(ordered):
    half_cols = ordered.shape[2] // 2
    return jnp.concatenate([-ordered[:, :, half_cols:], ordered[:, :, :half_cols]], axis=2)


def correlate_full(ordered, inverse_count):
    rotated = rotate_parts(ordered)
    real_vis = jnp.einsum("cak,cbk->cab", ordered, ordered, preferred_element_type=jnp.float32)
    imag_vis = jnp.einsum("cak,cbk->cab", ordered, rotated, preferred_element_type=jnp.float32)
    return (jnp.stack([real_vis, imag_vis], axis=0) * inverse_count).astype(jnp.bfloat16)


def local(samples, history, coefficients, station_of_slot, station_ok):
    tap_count, fft_len = coefficients.shape
    row_count = samples.shape[1]
    half_count = lax.axis_size("tch")
    block_count = lax.axis_size("blk")
    dest_count = half_count * block_count
    station_count = station_of_slot.shape[0]
    inner = fft_len // RADIX
    kl_count = inner // dest_count
    keep = row_count // half_count
    t = lax.axis_index("tch")
    blocks = samples.reshape(2, row_count, -1, fft_len)
    before = history.reshape(2, row_count, -1, fft_len)
    own = lax.dynamic_slice_in_dim(blocks, t * keep, keep, axis=1)
    other = lax.dynamic_slice_in_dim(blocks, (1 - t) * keep, keep, axis=1)
    received = lax.ppermute(other, "tch", [(0, 1), (1, 0)])
    is_first = t == 0
    first = jnp.where(is_first, own, received)
    second = jnp.where(is_first, received, own)
    earlier = lax.dynamic_slice_in_dim(before, t * keep, keep, axis=1)
    extended = jnp.concatenate([earlier, first, second], axis=2).reshape(2, keep, -1)
    spec_total = (extended.shape[2] - (tap_count - 1) * fft_len) // fft_len
    spectra = channelize(filter_bank(extended, coefficients, spec_total), 0.0 * coefficients[0, 0])
    spectra = spectra.reshape(dest_count, kl_count, -1)
    turned = lax.all_to_all(spectra, ("blk", "tch"), split_axis=0, concat_axis=0, tiled=True)
    slot_index = (
        jnp.zeros((station_count,), jnp.int32)
        .at[station_of_slot]
        .set(jnp.arange(station_count, dtype=jnp.int32))
    )
    chan_count = kl_count * RADIX
    input_count = station_count * POLS
    by_source = turned.reshape(station_count, kl_count, RADIX, POLS, 2 * spec_total)
    by_source = jnp.transpose(by_source, (1, 2, 3, 0, 4)).reshape(chan_count, input_count, 2 * spec_total)
    position = jnp.arange(input_count, dtype=jnp.int32)
    wanted = slot_index[position // POLS] + (position % POLS) * station_count
    select = (wanted[:, None] == position[None, :]).astype(turned.dtype)
    select = select * station_ok[position // POLS].astype(turned.dtype)[:, None]
    select = jnp.broadcast_to(select, (chan_count, input_count, input_count))
    ordered = jnp.einsum(
        "cij,cjk->cik", select, by_source, preferred_element_type=jnp.float32
    ).astype(turned.dtype)
    vis = correlate_full(ordered, 1.0 / spec_total)
    return with_layout_constraint(vis, Layout((0, 1, 2, 3)))


def solution(mesh):
    return jax.shard_map(
        local,
        mesh=mesh,
        in_specs=(P("grp", "blk", "tch"), P("grp", "blk", None), P(), P("grp"), P("grp")),
        out_specs=P("grp", ("blk", "tch"), None, None),
        check_vma=False,
    )
```

```python
import math

import numpy as np

import jax
import jax.numpy as jnp
from jax import lax
from jax.experimental.layout import Layout, with_layout_constraint
from jax.sharding import PartitionSpec as P

POLS = 2
RADIX = 4


def dft_tables(fft_len):
    inner = fft_len // RADIX
    n2 = np.arange(inner)
    k1 = np.arange(RADIX)
    tw_angle = 2.0 * np.pi * np.outer(k1, n2) / fft_len
    twiddle_re = np.cos(tw_angle).astype(np.float32)
    twiddle_im = (-np.sin(tw_angle)).astype(np.float32)
    angle = 2.0 * np.pi * (np.outer(n2, n2) % inner) / inner
    scale = 1.0 / math.sqrt(fft_len)
    inner_matrix = np.concatenate([np.cos(angle) * scale, np.sin(angle) * scale], axis=0)
    return twiddle_re, twiddle_im, inner_matrix.astype(np.float32)


def filter_bank(extended, coefficients, spec_count):
    tap_count, fft_len = coefficients.shape
    blocks = extended.reshape(extended.shape[0], extended.shape[1], -1, fft_len)
    weights = coefficients.reshape(tap_count, 1, fft_len)
    running = jnp.zeros((extended.shape[0], extended.shape[1], spec_count, fft_len), jnp.float32)
    for tap_index in range(tap_count):
        running = running + weights[tap_index] * blocks[
            :, :, tap_index : tap_index + spec_count, :
        ].astype(jnp.float32)
    return running.astype(jnp.bfloat16)


def channelize(filtered, origin):
    _, pol_count, spec_count, fft_len = filtered.shape
    inner = fft_len // RADIX
    twiddle_re, twiddle_im, inner_matrix = dft_tables(fft_len)
    x = filtered.astype(jnp.float32)
    xr = [x[0, :, :, j * inner : (j + 1) * inner] for j in range(RADIX)]
    xi = [x[1, :, :, j * inner : (j + 1) * inner] for j in range(RADIX)]
    ar, ai = xr[0] + xr[2], xi[0] + xi[2]
    br, bi = xr[1] + xr[3], xi[1] + xi[3]
    cr, ci = xr[0] - xr[2], xi[0] - xi[2]
    dr, di = xr[1] - xr[3], xi[1] - xi[3]
    yr = jnp.stack([ar + br, cr + di, ar - br, cr - di], axis=0)
    yi = jnp.stack([ai + bi, ci - dr, ai - bi, ci + dr], axis=0)
    angle = jnp.asarray(2.0 * np.pi * np.outer(np.arange(RADIX), np.arange(inner)) / fft_len, jnp.float32) + origin
    tr, ti, inner_matrix = lax.optimization_barrier(
        (jnp.cos(angle), -jnp.sin(angle), (jnp.asarray(inner_matrix) + origin).astype(jnp.bfloat16))
    )
    tr = tr[:, None, None, :]
    ti = ti[:, None, None, :]
    zr = yr * tr - yi * ti
    zi = yr * ti + yi * tr
    real_rows = jnp.concatenate([zr, zi], axis=-1)
    imag_rows = jnp.concatenate([zi, -zr], axis=-1)
    rows = jnp.stack([real_rows, imag_rows], axis=2).reshape(RADIX * pol_count * 2 * spec_count, 2 * inner)
    product = lax.dot_general(
        inner_matrix,
        rows.astype(jnp.bfloat16),
        (((0,), (1,)), ((), ())),
        preferred_element_type=jnp.float32,
    )
    return product.astype(jnp.bfloat16)


def rotate_parts(ordered):
    half_cols = ordered.shape[2] // 2
    return jnp.concatenate([-ordered[:, :, half_cols:], ordered[:, :, :half_cols]], axis=2)


def correlate_full(ordered, inverse_count):
    rotated = rotate_parts(ordered)
    real_vis = jnp.einsum("cak,cbk->cab", ordered, ordered, preferred_element_type=jnp.float32)
    imag_vis = jnp.einsum("cak,cbk->cab", ordered, rotated, preferred_element_type=jnp.float32)
    return (jnp.stack([real_vis, imag_vis], axis=0) * inverse_count).astype(jnp.bfloat16)


def local(samples, history, coefficients, station_of_slot, station_ok):
    tap_count, fft_len = coefficients.shape
    row_count = samples.shape[1]
    half_count = lax.axis_size("tch")
    block_count = lax.axis_size("blk")
    dest_count = half_count * block_count
    station_count = station_of_slot.shape[0]
    inner = fft_len // RADIX
    kl_count = inner // dest_count
    keep = row_count // half_count
    t = lax.axis_index("tch")
    blocks = samples.reshape(2, row_count, -1, fft_len)
    before = history.reshape(2, row_count, -1, fft_len)
    own = lax.dynamic_slice_in_dim(blocks, t * keep, keep, axis=1)
    other = lax.dynamic_slice_in_dim(blocks, (1 - t) * keep, keep, axis=1)
    received = lax.ppermute(other, "tch", [(0, 1), (1, 0)])
    is_first = t == 0
    first = jnp.where(is_first, own, received)
    second = jnp.where(is_first, received, own)
    earlier = lax.dynamic_slice_in_dim(before, t * keep, keep, axis=1)
    extended = jnp.concatenate([earlier, first, second], axis=2).reshape(2, keep, -1)
    spec_total = (extended.shape[2] - (tap_count - 1) * fft_len) // fft_len
    spectra = channelize(filter_bank(extended, coefficients, spec_total), 0.0 * coefficients[0, 0])
    spectra = spectra.reshape(dest_count, kl_count, -1)
    turned = lax.all_to_all(spectra, ("blk", "tch"), split_axis=0, concat_axis=0, tiled=True)
    slot_index = (
        jnp.zeros((station_count,), jnp.int32)
        .at[station_of_slot]
        .set(jnp.arange(station_count, dtype=jnp.int32))
    )
    chan_count = kl_count * RADIX
    input_count = station_count * POLS
    by_source = turned.reshape(station_count, kl_count, RADIX * POLS, 2 * spec_total)
    by_source = jnp.transpose(by_source, (1, 2, 0, 3)).reshape(chan_count, input_count, 2 * spec_total)
    position = jnp.arange(input_count, dtype=jnp.int32)
    wanted = slot_index[position // POLS] + (position % POLS) * station_count
    select = (wanted[:, None] == position[None, :]).astype(turned.dtype)
    select = select * station_ok[position // POLS].astype(turned.dtype)[:, None]
    select = jnp.broadcast_to(select, (chan_count, input_count, input_count))
    ordered = jnp.einsum(
        "cij,cjk->cik", select, by_source, preferred_element_type=jnp.float32
    ).astype(turned.dtype)
    vis = correlate_full(ordered, 1.0 / spec_total)
    return with_layout_constraint(vis, Layout((0, 1, 2, 3)))


def solution(mesh):
    return jax.shard_map(
        local,
        mesh=mesh,
        in_specs=(P("grp", "blk", "tch"), P("grp", "blk", None), P(), P("grp"), P("grp")),
        out_specs=P("grp", ("blk", "tch"), None, None),
        check_vma=False,
    )
```

```python
import math

import numpy as np

import jax
import jax.numpy as jnp
from jax import lax
from jax.experimental.layout import Layout, with_layout_constraint
from jax.sharding import PartitionSpec as P

POLS = 2
RADIX = 4


def dft_tables(fft_len):
    inner = fft_len // RADIX
    n2 = np.arange(inner)
    k1 = np.arange(RADIX)
    tw_angle = 2.0 * np.pi * np.outer(k1, n2) / fft_len
    twiddle_re = np.cos(tw_angle).astype(np.float32)
    twiddle_im = (-np.sin(tw_angle)).astype(np.float32)
    angle = 2.0 * np.pi * (np.outer(n2, n2) % inner) / inner
    scale = 1.0 / math.sqrt(fft_len)
    inner_matrix = np.concatenate([np.cos(angle) * scale, np.sin(angle) * scale], axis=0)
    return twiddle_re, twiddle_im, inner_matrix.astype(np.float32)


def filter_bank(extended, coefficients, spec_count):
    tap_count, fft_len = coefficients.shape
    blocks = extended.reshape(extended.shape[0], extended.shape[1], -1, fft_len)
    weights = coefficients.reshape(tap_count, 1, fft_len)
    running = jnp.zeros((extended.shape[0], extended.shape[1], spec_count, fft_len), jnp.float32)
    for tap_index in range(tap_count):
        running = running + weights[tap_index] * blocks[
            :, :, tap_index : tap_index + spec_count, :
        ].astype(jnp.float32)
    return running.astype(jnp.bfloat16)


def channelize(filtered, origin):
    _, pol_count, spec_count, fft_len = filtered.shape
    inner = fft_len // RADIX
    twiddle_re, twiddle_im, inner_matrix = dft_tables(fft_len)
    x = filtered.astype(jnp.float32)
    xr = [x[0, :, :, j * inner : (j + 1) * inner] for j in range(RADIX)]
    xi = [x[1, :, :, j * inner : (j + 1) * inner] for j in range(RADIX)]
    ar, ai = xr[0] + xr[2], xi[0] + xi[2]
    br, bi = xr[1] + xr[3], xi[1] + xi[3]
    cr, ci = xr[0] - xr[2], xi[0] - xi[2]
    dr, di = xr[1] - xr[3], xi[1] - xi[3]
    yr = jnp.stack([ar + br, cr + di, ar - br, cr - di], axis=0)
    yi = jnp.stack([ai + bi, ci - dr, ai - bi, ci + dr], axis=0)
    angle = jnp.asarray(2.0 * np.pi * np.outer(np.arange(RADIX), np.arange(inner)) / fft_len, jnp.float32) + origin
    tr, ti, inner_matrix = lax.optimization_barrier(
        (jnp.cos(angle), -jnp.sin(angle), (jnp.asarray(inner_matrix) + origin).astype(jnp.bfloat16))
    )
    tr = tr[:, None, None, :]
    ti = ti[:, None, None, :]
    zr = yr * tr - yi * ti
    zi = yr * ti + yi * tr
    real_rows = jnp.concatenate([zr, zi], axis=-1)
    imag_rows = jnp.concatenate([zi, -zr], axis=-1)
    rows = jnp.stack([real_rows, imag_rows], axis=2).reshape(RADIX * pol_count * 2 * spec_count, 2 * inner)
    product = lax.dot_general(
        inner_matrix,
        rows.astype(jnp.bfloat16),
        (((0,), (1,)), ((), ())),
        preferred_element_type=jnp.float32,
    )
    return product.astype(jnp.bfloat16)


def rotate_parts(ordered):
    half_cols = ordered.shape[2] // 2
    return jnp.concatenate([-ordered[:, :, half_cols:], ordered[:, :, :half_cols]], axis=2)


def correlate_full(ordered, inverse_count):
    rotated = rotate_parts(ordered)
    real_vis = jnp.einsum("cak,cbk->cab", ordered, ordered, preferred_element_type=jnp.float32)
    imag_vis = jnp.einsum("cak,cbk->cab", ordered, rotated, preferred_element_type=jnp.float32)
    return (jnp.stack([real_vis, imag_vis], axis=0) * inverse_count).astype(jnp.bfloat16)


def local(samples, history, coefficients, station_of_slot, station_ok):
    tap_count, fft_len = coefficients.shape
    row_count = samples.shape[1]
    half_count = lax.axis_size("tch")
    block_count = lax.axis_size("blk")
    dest_count = half_count * block_count
    station_count = station_of_slot.shape[0]
    inner = fft_len // RADIX
    kl_count = inner // dest_count
    keep = row_count // half_count
    t = lax.axis_index("tch")
    blocks = samples.reshape(2, row_count, -1, fft_len)
    before = history.reshape(2, row_count, -1, fft_len)
    own = lax.dynamic_slice_in_dim(blocks, t * keep, keep, axis=1)
    other = lax.dynamic_slice_in_dim(blocks, (1 - t) * keep, keep, axis=1)
    received = jnp.concatenate(
        [lax.ppermute(other[part : part + 1], "tch", [(0, 1), (1, 0)]) for part in range(2)], axis=0
    )
    is_first = t == 0
    first = jnp.where(is_first, own, received)
    second = jnp.where(is_first, received, own)
    earlier = lax.dynamic_slice_in_dim(before, t * keep, keep, axis=1)
    extended = jnp.concatenate([earlier, first, second], axis=2).reshape(2, keep, -1)
    spec_total = (extended.shape[2] - (tap_count - 1) * fft_len) // fft_len
    spectra = channelize(filter_bank(extended, coefficients, spec_total), 0.0 * coefficients[0, 0])
    spectra = spectra.reshape(dest_count, kl_count, -1)
    turned = lax.all_to_all(spectra, ("blk", "tch"), split_axis=0, concat_axis=0, tiled=True)
    slot_index = (
        jnp.zeros((station_count,), jnp.int32)
        .at[station_of_slot]
        .set(jnp.arange(station_count, dtype=jnp.int32))
    )
    chan_count = kl_count * RADIX
    input_count = station_count * POLS
    by_source = turned.reshape(station_count, kl_count, RADIX * POLS, 2 * spec_total)
    by_source = jnp.transpose(by_source, (1, 2, 0, 3)).reshape(chan_count, input_count, 2 * spec_total)
    position = jnp.arange(input_count, dtype=jnp.int32)
    wanted = slot_index[position // POLS] + (position % POLS) * station_count
    select = (wanted[:, None] == position[None, :]).astype(turned.dtype)
    select = select * station_ok[position // POLS].astype(turned.dtype)[:, None]
    select = jnp.broadcast_to(select, (chan_count, input_count, input_count))
    ordered = jnp.einsum(
        "cij,cjk->cik", select, by_source, preferred_element_type=jnp.float32
    ).astype(turned.dtype)
    vis = correlate_full(ordered, 1.0 / spec_total)
    return with_layout_constraint(vis, Layout((0, 1, 2, 3)))


def solution(mesh):
    return jax.shard_map(
        local,
        mesh=mesh,
        in_specs=(P("grp", "blk", "tch"), P("grp", "blk", None), P(), P("grp"), P("grp")),
        out_specs=P("grp", ("blk", "tch"), None, None),
        check_vma=False,
    )
```

```python
import math

import numpy as np

import jax
import jax.numpy as jnp
from jax import lax
from jax.experimental.layout import Layout, with_layout_constraint
from jax.sharding import PartitionSpec as P

POLS = 2
RADIX = 4


def dft_tables(fft_len):
    inner = fft_len // RADIX
    n2 = np.arange(inner)
    k1 = np.arange(RADIX)
    tw_angle = 2.0 * np.pi * np.outer(k1, n2) / fft_len
    twiddle_re = np.cos(tw_angle).astype(np.float32)
    twiddle_im = (-np.sin(tw_angle)).astype(np.float32)
    angle = 2.0 * np.pi * (np.outer(n2, n2) % inner) / inner
    scale = 1.0 / math.sqrt(fft_len)
    inner_matrix = np.concatenate([np.cos(angle) * scale, np.sin(angle) * scale], axis=0)
    return twiddle_re, twiddle_im, inner_matrix.astype(np.float32)


def filter_bank(extended, coefficients, spec_count):
    tap_count, fft_len = coefficients.shape
    blocks = extended.reshape(extended.shape[0], extended.shape[1], -1, fft_len)
    weights = coefficients.reshape(tap_count, 1, fft_len)
    running = jnp.zeros((extended.shape[0], extended.shape[1], spec_count, fft_len), jnp.float32)
    for tap_index in range(tap_count):
        running = running + weights[tap_index] * blocks[
            :, :, tap_index : tap_index + spec_count, :
        ].astype(jnp.float32)
    return running.astype(jnp.bfloat16)


def channelize(filtered, origin):
    _, pol_count, spec_count, fft_len = filtered.shape
    inner = fft_len // RADIX
    twiddle_re, twiddle_im, inner_matrix = dft_tables(fft_len)
    x = filtered.astype(jnp.float32)
    xr = [x[0, :, :, j * inner : (j + 1) * inner] for j in range(RADIX)]
    xi = [x[1, :, :, j * inner : (j + 1) * inner] for j in range(RADIX)]
    ar, ai = xr[0] + xr[2], xi[0] + xi[2]
    br, bi = xr[1] + xr[3], xi[1] + xi[3]
    cr, ci = xr[0] - xr[2], xi[0] - xi[2]
    dr, di = xr[1] - xr[3], xi[1] - xi[3]
    yr = jnp.stack([ar + br, cr + di, ar - br, cr - di], axis=0)
    yi = jnp.stack([ai + bi, ci - dr, ai - bi, ci + dr], axis=0)
    angle = jnp.asarray(2.0 * np.pi * np.outer(np.arange(RADIX), np.arange(inner)) / fft_len, jnp.float32) + origin
    tr, ti, inner_matrix = lax.optimization_barrier(
        (jnp.cos(angle), -jnp.sin(angle), jnp.asarray(inner_matrix, jnp.bfloat16) + origin.astype(jnp.bfloat16))
    )
    tr = tr[:, None, None, :]
    ti = ti[:, None, None, :]
    zr = yr * tr - yi * ti
    zi = yr * ti + yi * tr
    real_rows = jnp.concatenate([zr, zi], axis=-1)
    imag_rows = jnp.concatenate([zi, -zr], axis=-1)
    rows = jnp.stack([real_rows, imag_rows], axis=2).reshape(RADIX * pol_count * 2 * spec_count, 2 * inner)
    product = lax.dot_general(
        inner_matrix,
        rows.astype(jnp.bfloat16),
        (((0,), (1,)), ((), ())),
        preferred_element_type=jnp.float32,
    )
    return product.astype(jnp.bfloat16)


def rotate_parts(ordered):
    half_cols = ordered.shape[2] // 2
    return jnp.concatenate([-ordered[:, :, half_cols:], ordered[:, :, :half_cols]], axis=2)


def correlate_full(ordered, inverse_count):
    rotated = rotate_parts(ordered)
    real_vis = jnp.einsum("cak,cbk->cab", ordered, ordered, preferred_element_type=jnp.float32)
    imag_vis = jnp.einsum("cak,cbk->cab", ordered, rotated, preferred_element_type=jnp.float32)
    return (jnp.stack([real_vis, imag_vis], axis=0) * inverse_count).astype(jnp.bfloat16)


def local(samples, history, coefficients, station_of_slot, station_ok):
    tap_count, fft_len = coefficients.shape
    row_count = samples.shape[1]
    half_count = lax.axis_size("tch")
    block_count = lax.axis_size("blk")
    dest_count = half_count * block_count
    station_count = station_of_slot.shape[0]
    inner = fft_len // RADIX
    kl_count = inner // dest_count
    keep = row_count // half_count
    t = lax.axis_index("tch")
    blocks = samples.reshape(2, row_count, -1, fft_len)
    before = history.reshape(2, row_count, -1, fft_len)
    own = lax.dynamic_slice_in_dim(blocks, t * keep, keep, axis=1)
    other = lax.dynamic_slice_in_dim(blocks, (1 - t) * keep, keep, axis=1)
    received = lax.ppermute(other, "tch", [(0, 1), (1, 0)])
    is_first = t == 0
    first = jnp.where(is_first, own, received)
    second = jnp.where(is_first, received, own)
    earlier = lax.dynamic_slice_in_dim(before, t * keep, keep, axis=1)
    extended = jnp.concatenate([earlier, first, second], axis=2).reshape(2, keep, -1)
    spec_total = (extended.shape[2] - (tap_count - 1) * fft_len) // fft_len
    spectra = channelize(filter_bank(extended, coefficients, spec_total), 0.0 * coefficients[0, 0])
    spectra = spectra.reshape(dest_count, kl_count, -1)
    turned = lax.all_to_all(spectra, ("blk", "tch"), split_axis=0, concat_axis=0, tiled=True)
    slot_index = (
        jnp.zeros((station_count,), jnp.int32)
        .at[station_of_slot]
        .set(jnp.arange(station_count, dtype=jnp.int32))
    )
    chan_count = kl_count * RADIX
    input_count = station_count * POLS
    by_source = turned.reshape(station_count, kl_count, RADIX * POLS, 2 * spec_total)
    by_source = jnp.transpose(by_source, (1, 2, 0, 3)).reshape(chan_count, input_count, 2 * spec_total)
    position = jnp.arange(input_count, dtype=jnp.int32)
    wanted = slot_index[position // POLS] + (position % POLS) * station_count
    select = (wanted[:, None] == position[None, :]).astype(turned.dtype)
    select = select * station_ok[position // POLS].astype(turned.dtype)[:, None]
    select = jnp.broadcast_to(select, (chan_count, input_count, input_count))
    ordered = jnp.einsum(
        "cij,cjk->cik", select, by_source, preferred_element_type=jnp.float32
    ).astype(turned.dtype)
    vis = correlate_full(ordered, 1.0 / spec_total)
    return with_layout_constraint(vis, Layout((0, 1, 2, 3)))


def solution(mesh):
    return jax.shard_map(
        local,
        mesh=mesh,
        in_specs=(P("grp", "blk", "tch"), P("grp", "blk", None), P(), P("grp"), P("grp")),
        out_specs=P("grp", ("blk", "tch"), None, None),
        check_vma=False,
    )
```

```python
import math

import numpy as np

import jax
import jax.numpy as jnp
from jax import lax
from jax.experimental.layout import Layout, with_layout_constraint
from jax.sharding import PartitionSpec as P

POLS = 2
RADIX = 4


def dft_tables(fft_len):
    inner = fft_len // RADIX
    n2 = np.arange(inner)
    k1 = np.arange(RADIX)
    tw_angle = 2.0 * np.pi * np.outer(k1, n2) / fft_len
    twiddle_re = np.cos(tw_angle).astype(np.float32)
    twiddle_im = (-np.sin(tw_angle)).astype(np.float32)
    angle = 2.0 * np.pi * (np.outer(n2, n2) % inner) / inner
    scale = 1.0 / math.sqrt(fft_len)
    inner_matrix = np.concatenate([np.cos(angle) * scale, np.sin(angle) * scale], axis=0)
    return twiddle_re, twiddle_im, inner_matrix.astype(np.float32)


def filter_bank(extended, coefficients, spec_count):
    tap_count, fft_len = coefficients.shape
    blocks = extended.reshape(extended.shape[0], extended.shape[1], -1, fft_len)
    weights = coefficients.reshape(tap_count, 1, fft_len)
    running = jnp.zeros((extended.shape[0], extended.shape[1], spec_count, fft_len), jnp.float32)
    for tap_index in range(tap_count):
        running = running + weights[tap_index] * blocks[
            :, :, tap_index : tap_index + spec_count, :
        ].astype(jnp.float32)
    return running.astype(jnp.bfloat16)


def channelize(filtered, origin):
    _, pol_count, spec_count, fft_len = filtered.shape
    inner = fft_len // RADIX
    twiddle_re, twiddle_im, inner_matrix = dft_tables(fft_len)
    x = filtered.astype(jnp.float32)
    xr = [x[0, :, :, j * inner : (j + 1) * inner] for j in range(RADIX)]
    xi = [x[1, :, :, j * inner : (j + 1) * inner] for j in range(RADIX)]
    ar, ai = xr[0] + xr[2], xi[0] + xi[2]
    br, bi = xr[1] + xr[3], xi[1] + xi[3]
    cr, ci = xr[0] - xr[2], xi[0] - xi[2]
    dr, di = xr[1] - xr[3], xi[1] - xi[3]
    yr = jnp.stack([ar + br, cr + di, ar - br, cr - di], axis=0)
    yi = jnp.stack([ai + bi, ci - dr, ai - bi, ci + dr], axis=0)
    angle = jnp.asarray(2.0 * np.pi * np.outer(np.arange(RADIX), np.arange(inner)) / fft_len, jnp.float32) + origin
    tr, ti, inner_matrix = lax.optimization_barrier(
        (jnp.cos(angle), -jnp.sin(angle), jnp.asarray(inner_matrix, jnp.bfloat16) + origin.astype(jnp.bfloat16))
    )
    tr = tr[:, None, None, :]
    ti = ti[:, None, None, :]
    zr = yr * tr - yi * ti
    zi = yr * ti + yi * tr
    real_rows = jnp.concatenate([zr, zi], axis=-1)
    imag_rows = jnp.concatenate([zi, -zr], axis=-1)
    rows = jnp.stack([real_rows, imag_rows], axis=2).reshape(RADIX * pol_count * 2 * spec_count, 2 * inner)
    product = lax.dot_general(
        inner_matrix,
        rows.astype(jnp.bfloat16),
        (((0,), (1,)), ((), ())),
        preferred_element_type=jnp.float32,
    )
    return product.astype(jnp.bfloat16)


def correlate_full(ordered, inverse_count, half_count):
    width = ordered.shape[2]
    half = width // 2
    turn = np.zeros((width, width), np.float32)
    turn[half + np.arange(half), np.arange(half)] = -1.0
    turn[np.arange(half), half + np.arange(half)] = 1.0
    rotated = jnp.einsum(
        "cak,kj->caj", ordered, jnp.asarray(turn, ordered.dtype), preferred_element_type=jnp.float32
    ).astype(ordered.dtype)
    real_vis = jnp.einsum("cak,cbk->cab", ordered, ordered, preferred_element_type=jnp.float32)
    imag_vis = jnp.einsum("cak,cbk->cab", ordered, rotated, preferred_element_type=jnp.float32)
    chan_count = ordered.shape[0] // half_count
    real_vis = real_vis.reshape(half_count, chan_count, *real_vis.shape[1:]).sum(axis=0)
    imag_vis = imag_vis.reshape(half_count, chan_count, *imag_vis.shape[1:]).sum(axis=0)
    return (jnp.stack([real_vis, imag_vis], axis=0) * inverse_count).astype(jnp.bfloat16)


def local(samples, history, coefficients, station_of_slot, station_ok):
    tap_count, fft_len = coefficients.shape
    row_count = samples.shape[1]
    half_count = lax.axis_size("tch")
    block_count = lax.axis_size("blk")
    dest_count = half_count * block_count
    station_count = station_of_slot.shape[0]
    inner = fft_len // RADIX
    kl_count = inner // dest_count
    keep = row_count // half_count
    t = lax.axis_index("tch")
    tail = samples[:, :, samples.shape[2] - (tap_count - 1) * fft_len :]
    from_previous = lax.ppermute(tail, "tch", [(0, 1)])
    earlier = jnp.where(t == 0, history, from_previous)
    extended = jnp.concatenate([earlier, samples], axis=2)
    spec_local = (extended.shape[2] - (tap_count - 1) * fft_len) // fft_len
    spec_total = spec_local * half_count
    spectra = channelize(filter_bank(extended, coefficients, spec_local), 0.0 * coefficients[0, 0])
    spectra = spectra.reshape(dest_count, kl_count, -1)
    turned = lax.all_to_all(spectra, ("blk", "tch"), split_axis=0, concat_axis=0, tiled=True)
    slot_index = (
        jnp.zeros((station_count,), jnp.int32)
        .at[station_of_slot]
        .set(jnp.arange(station_count, dtype=jnp.int32))
    )
    chan_count = kl_count * RADIX
    input_count = station_count * POLS
    by_source = turned.reshape(block_count, half_count, kl_count, RADIX, row_count, 2 * spec_local)
    by_source = jnp.transpose(by_source, (1, 2, 3, 0, 4, 5)).reshape(
        half_count * chan_count, input_count, 2 * spec_local
    )
    position = jnp.arange(input_count, dtype=jnp.int32)
    wanted = slot_index[position // POLS] * POLS + position % POLS
    select = (wanted[:, None] == position[None, :]).astype(turned.dtype)
    select = select * station_ok[position // POLS].astype(turned.dtype)[:, None]
    select = jnp.broadcast_to(select, (half_count * chan_count, input_count, input_count))
    ordered = jnp.einsum(
        "cij,cjk->cik", select, by_source, preferred_element_type=jnp.float32
    ).astype(turned.dtype)
    vis = correlate_full(ordered, 1.0 / spec_total, half_count)
    return with_layout_constraint(vis, Layout((0, 1, 2, 3)))


def solution(mesh):
    return jax.shard_map(
        local,
        mesh=mesh,
        in_specs=(P("grp", "blk", "tch"), P("grp", "blk", None), P(), P("grp"), P("grp")),
        out_specs=P("grp", ("blk", "tch"), None, None),
        check_vma=False,
    )
```

```python
import math

import numpy as np

import jax
import jax.numpy as jnp
from jax import lax
from jax.experimental.layout import Layout, with_layout_constraint
from jax.sharding import PartitionSpec as P

POLS = 2
RADIX = 4


def dft_tables(fft_len):
    inner = fft_len // RADIX
    n2 = np.arange(inner)
    k1 = np.arange(RADIX)
    tw_angle = 2.0 * np.pi * np.outer(k1, n2) / fft_len
    twiddle_re = np.cos(tw_angle).astype(np.float32)
    twiddle_im = (-np.sin(tw_angle)).astype(np.float32)
    angle = 2.0 * np.pi * (np.outer(n2, n2) % inner) / inner
    scale = 1.0 / math.sqrt(fft_len)
    inner_matrix = np.concatenate([np.cos(angle) * scale, np.sin(angle) * scale], axis=0)
    return twiddle_re, twiddle_im, inner_matrix.astype(np.float32)


def filter_bank(extended, coefficients, spec_count):
    tap_count, fft_len = coefficients.shape
    blocks = extended.reshape(extended.shape[0], extended.shape[1], -1, fft_len)
    weights = coefficients.reshape(tap_count, 1, fft_len)
    running = jnp.zeros((extended.shape[0], extended.shape[1], spec_count, fft_len), jnp.float32)
    for tap_index in range(tap_count):
        running = running + weights[tap_index] * blocks[
            :, :, tap_index : tap_index + spec_count, :
        ].astype(jnp.float32)
    return running.astype(jnp.bfloat16)


def channelize(filtered, origin):
    _, pol_count, spec_count, fft_len = filtered.shape
    inner = fft_len // RADIX
    twiddle_re, twiddle_im, inner_matrix = dft_tables(fft_len)
    x = filtered.astype(jnp.float32)
    xr = [x[0, :, :, j * inner : (j + 1) * inner] for j in range(RADIX)]
    xi = [x[1, :, :, j * inner : (j + 1) * inner] for j in range(RADIX)]
    ar, ai = xr[0] + xr[2], xi[0] + xi[2]
    br, bi = xr[1] + xr[3], xi[1] + xi[3]
    cr, ci = xr[0] - xr[2], xi[0] - xi[2]
    dr, di = xr[1] - xr[3], xi[1] - xi[3]
    yr = jnp.stack([ar + br, cr + di, ar - br, cr - di], axis=0)
    yi = jnp.stack([ai + bi, ci - dr, ai - bi, ci + dr], axis=0)
    angle = jnp.asarray(2.0 * np.pi * np.outer(np.arange(RADIX), np.arange(inner)) / fft_len, jnp.float32) + origin
    tr, ti, inner_matrix = lax.optimization_barrier(
        (jnp.cos(angle), -jnp.sin(angle), jnp.asarray(inner_matrix, jnp.bfloat16) + origin.astype(jnp.bfloat16))
    )
    tr = tr[:, None, None, :]
    ti = ti[:, None, None, :]
    zr = yr * tr - yi * ti
    zi = yr * ti + yi * tr
    real_rows = jnp.concatenate([zr, zi], axis=-1)
    imag_rows = jnp.concatenate([zi, -zr], axis=-1)
    rows = jnp.stack([real_rows, imag_rows], axis=2).reshape(RADIX * pol_count * 2 * spec_count, 2 * inner)
    product = lax.dot_general(
        inner_matrix,
        rows.astype(jnp.bfloat16),
        (((0,), (1,)), ((), ())),
        preferred_element_type=jnp.float32,
    )
    return product.astype(jnp.bfloat16)


def rotate_parts(ordered):
    half_cols = ordered.shape[2] // 2
    return jnp.concatenate([-ordered[:, :, half_cols:], ordered[:, :, :half_cols]], axis=2)


def correlate_full(ordered, inverse_count):
    half_cols = ordered.shape[2] // 2
    real_vis = jnp.einsum("cak,cbk->cab", ordered, ordered, preferred_element_type=jnp.float32)
    cross = jnp.einsum(
        "cak,cbk->cab", ordered[:, :, half_cols:], ordered[:, :, :half_cols], preferred_element_type=jnp.float32
    )
    imag_vis = cross - jnp.swapaxes(cross, 1, 2)
    return (jnp.stack([real_vis, imag_vis], axis=0) * inverse_count).astype(jnp.bfloat16)


def local(samples, history, coefficients, station_of_slot, station_ok):
    tap_count, fft_len = coefficients.shape
    row_count = samples.shape[1]
    half_count = lax.axis_size("tch")
    block_count = lax.axis_size("blk")
    dest_count = half_count * block_count
    station_count = station_of_slot.shape[0]
    inner = fft_len // RADIX
    kl_count = inner // dest_count
    keep = row_count // half_count
    t = lax.axis_index("tch")
    blocks = samples.reshape(2, row_count, -1, fft_len)
    before = history.reshape(2, row_count, -1, fft_len)
    own = lax.dynamic_slice_in_dim(blocks, t * keep, keep, axis=1)
    other = lax.dynamic_slice_in_dim(blocks, (1 - t) * keep, keep, axis=1)
    received = lax.ppermute(other, "tch", [(0, 1), (1, 0)])
    is_first = t == 0
    first = jnp.where(is_first, own, received)
    second = jnp.where(is_first, received, own)
    earlier = lax.dynamic_slice_in_dim(before, t * keep, keep, axis=1)
    extended = jnp.concatenate([earlier, first, second], axis=2).reshape(2, keep, -1)
    spec_total = (extended.shape[2] - (tap_count - 1) * fft_len) // fft_len
    spectra = channelize(filter_bank(extended, coefficients, spec_total), 0.0 * coefficients[0, 0])
    spectra = spectra.reshape(dest_count, kl_count, -1)
    turned = lax.all_to_all(spectra, ("blk", "tch"), split_axis=0, concat_axis=0, tiled=True)
    slot_index = (
        jnp.zeros((station_count,), jnp.int32)
        .at[station_of_slot]
        .set(jnp.arange(station_count, dtype=jnp.int32))
    )
    chan_count = kl_count * RADIX
    input_count = station_count * POLS
    by_source = turned.reshape(station_count, kl_count, RADIX * POLS, 2 * spec_total)
    by_source = jnp.transpose(by_source, (1, 2, 0, 3)).reshape(chan_count, input_count, 2 * spec_total)
    position = jnp.arange(input_count, dtype=jnp.int32)
    wanted = slot_index[position // POLS] + (position % POLS) * station_count
    select = (wanted[:, None] == position[None, :]).astype(turned.dtype)
    select = select * station_ok[position // POLS].astype(turned.dtype)[:, None]
    select = jnp.broadcast_to(select, (chan_count, input_count, input_count))
    ordered = jnp.einsum(
        "cij,cjk->cik", select, by_source, preferred_element_type=jnp.float32
    ).astype(turned.dtype)
    vis = correlate_full(ordered, 1.0 / spec_total)
    return with_layout_constraint(vis, Layout((0, 1, 2, 3)))


def solution(mesh):
    return jax.shard_map(
        local,
        mesh=mesh,
        in_specs=(P("grp", "blk", "tch"), P("grp", "blk", None), P(), P("grp"), P("grp")),
        out_specs=P("grp", ("blk", "tch"), None, None),
        check_vma=False,
    )
```

```python
import math

import numpy as np

import jax
import jax.numpy as jnp
from jax import lax
from jax.experimental.layout import Layout, with_layout_constraint
from jax.sharding import PartitionSpec as P

POLS = 2
RADIX = 4


def dft_tables(fft_len):
    inner = fft_len // RADIX
    n2 = np.arange(inner)
    k1 = np.arange(RADIX)
    tw_angle = 2.0 * np.pi * np.outer(k1, n2) / fft_len
    twiddle_re = np.cos(tw_angle).astype(np.float32)
    twiddle_im = (-np.sin(tw_angle)).astype(np.float32)
    angle = 2.0 * np.pi * (np.outer(n2, n2) % inner) / inner
    scale = 1.0 / math.sqrt(fft_len)
    inner_matrix = np.concatenate([np.cos(angle) * scale, np.sin(angle) * scale], axis=0)
    return twiddle_re, twiddle_im, inner_matrix.astype(np.float32)


def filter_bank(extended, coefficients, spec_count):
    tap_count, fft_len = coefficients.shape
    blocks = extended.reshape(extended.shape[0], extended.shape[1], -1, fft_len)
    weights = coefficients.reshape(tap_count, 1, fft_len)
    running = jnp.zeros((extended.shape[0], extended.shape[1], spec_count, fft_len), jnp.float32)
    for tap_index in range(tap_count):
        running = running + weights[tap_index] * blocks[
            :, :, tap_index : tap_index + spec_count, :
        ].astype(jnp.float32)
    return running.astype(jnp.bfloat16)


def channelize(filtered, origin):
    _, pol_count, spec_count, fft_len = filtered.shape
    inner = fft_len // RADIX
    twiddle_re, twiddle_im, inner_matrix = dft_tables(fft_len)
    x = filtered.astype(jnp.float32)
    xr = [x[0, :, :, j * inner : (j + 1) * inner] for j in range(RADIX)]
    xi = [x[1, :, :, j * inner : (j + 1) * inner] for j in range(RADIX)]
    ar, ai = xr[0] + xr[2], xi[0] + xi[2]
    br, bi = xr[1] + xr[3], xi[1] + xi[3]
    cr, ci = xr[0] - xr[2], xi[0] - xi[2]
    dr, di = xr[1] - xr[3], xi[1] - xi[3]
    yr = jnp.stack([ar + br, cr + di, ar - br, cr - di], axis=0)
    yi = jnp.stack([ai + bi, ci - dr, ai - bi, ci + dr], axis=0)
    angle = jnp.asarray(2.0 * np.pi * np.outer(np.arange(RADIX), np.arange(inner)) / fft_len, jnp.float32) + origin
    tr, ti, inner_matrix = lax.optimization_barrier(
        (jnp.cos(angle), -jnp.sin(angle), jnp.asarray(inner_matrix, jnp.bfloat16) + origin.astype(jnp.bfloat16))
    )
    tr = tr[:, None, None, :]
    ti = ti[:, None, None, :]
    zr = yr * tr - yi * ti
    zi = yr * ti + yi * tr
    real_rows = jnp.concatenate([zr, zi], axis=-1)
    imag_rows = jnp.concatenate([zi, -zr], axis=-1)
    rows = jnp.stack([real_rows, imag_rows], axis=2).reshape(RADIX * pol_count * 2 * spec_count, 2 * inner)
    product = lax.dot_general(
        inner_matrix,
        rows.astype(jnp.bfloat16),
        (((0,), (1,)), ((), ())),
        preferred_element_type=jnp.float32,
    )
    return product.astype(jnp.bfloat16)


def rotate_parts(ordered):
    half_cols = ordered.shape[2] // 2
    return jnp.concatenate([-ordered[:, :, half_cols:], ordered[:, :, :half_cols]], axis=2)


def correlate_full(ordered, inverse_count):
    rotated = rotate_parts(ordered)
    real_vis = jnp.einsum("cak,cbk->cab", ordered, ordered, preferred_element_type=jnp.float32)
    imag_vis = jnp.einsum("cak,cbk->cab", ordered, rotated, preferred_element_type=jnp.float32)
    return (jnp.stack([real_vis, imag_vis], axis=0) * inverse_count).astype(jnp.bfloat16)


def local(samples, history, coefficients, station_of_slot, station_ok):
    tap_count, fft_len = coefficients.shape
    row_count = samples.shape[1]
    half_count = lax.axis_size("tch")
    block_count = lax.axis_size("blk")
    dest_count = half_count * block_count
    station_count = station_of_slot.shape[0]
    inner = fft_len // RADIX
    kl_count = inner // dest_count
    keep = row_count // half_count
    t = lax.axis_index("tch")
    blocks = samples.astype(jnp.float32).reshape(2, row_count, -1, fft_len)
    before = history.astype(jnp.float32).reshape(2, row_count, -1, fft_len)
    own = lax.dynamic_slice_in_dim(blocks, t * keep, keep, axis=1)
    other = lax.dynamic_slice_in_dim(blocks, (1 - t) * keep, keep, axis=1)
    received = lax.ppermute(other, "tch", [(0, 1), (1, 0)])
    is_first = t == 0
    first = jnp.where(is_first, own, received)
    second = jnp.where(is_first, received, own)
    earlier = lax.dynamic_slice_in_dim(before, t * keep, keep, axis=1)
    extended = jnp.concatenate([earlier, first, second], axis=2).reshape(2, keep, -1)
    spec_total = (extended.shape[2] - (tap_count - 1) * fft_len) // fft_len
    spectra = channelize(filter_bank(extended, coefficients, spec_total), 0.0 * coefficients[0, 0])
    spectra = spectra.reshape(dest_count, kl_count, -1)
    turned = lax.all_to_all(spectra, ("blk", "tch"), split_axis=0, concat_axis=0, tiled=True)
    slot_index = (
        jnp.zeros((station_count,), jnp.int32)
        .at[station_of_slot]
        .set(jnp.arange(station_count, dtype=jnp.int32))
    )
    chan_count = kl_count * RADIX
    input_count = station_count * POLS
    by_source = turned.reshape(station_count, kl_count, RADIX * POLS, 2 * spec_total)
    by_source = jnp.transpose(by_source, (1, 2, 0, 3)).reshape(chan_count, input_count, 2 * spec_total)
    position = jnp.arange(input_count, dtype=jnp.int32)
    wanted = slot_index[position // POLS] + (position % POLS) * station_count
    select = (wanted[:, None] == position[None, :]).astype(turned.dtype)
    select = select * station_ok[position // POLS].astype(turned.dtype)[:, None]
    select = jnp.broadcast_to(select, (chan_count, input_count, input_count))
    ordered = jnp.einsum(
        "cij,cjk->cik", select, by_source, preferred_element_type=jnp.float32
    ).astype(turned.dtype)
    vis = correlate_full(ordered, 1.0 / spec_total)
    return with_layout_constraint(vis, Layout((0, 1, 2, 3)))


def solution(mesh):
    return jax.shard_map(
        local,
        mesh=mesh,
        in_specs=(P("grp", "blk", "tch"), P("grp", "blk", None), P(), P("grp"), P("grp")),
        out_specs=P("grp", ("blk", "tch"), None, None),
        check_vma=False,
    )
```

```python
import math

import numpy as np

import jax
import jax.numpy as jnp
from jax import lax
from jax.experimental.layout import Layout, with_layout_constraint
from jax.sharding import PartitionSpec as P

POLS = 2
RADIX = 4


def dft_tables(fft_len):
    inner = fft_len // RADIX
    n2 = np.arange(inner)
    k1 = np.arange(RADIX)
    tw_angle = 2.0 * np.pi * np.outer(k1, n2) / fft_len
    twiddle_re = np.cos(tw_angle).astype(np.float32)
    twiddle_im = (-np.sin(tw_angle)).astype(np.float32)
    angle = 2.0 * np.pi * (np.outer(n2, n2) % inner) / inner
    scale = 1.0 / math.sqrt(fft_len)
    inner_matrix = np.concatenate([np.cos(angle) * scale, np.sin(angle) * scale], axis=0)
    return twiddle_re, twiddle_im, inner_matrix.astype(np.float32)


def filter_bank(extended, coefficients, spec_count):
    tap_count, fft_len = coefficients.shape
    blocks = extended.reshape(extended.shape[0], extended.shape[1], -1, fft_len)
    weights = coefficients.reshape(tap_count, 1, fft_len)
    running = jnp.zeros((extended.shape[0], extended.shape[1], spec_count, fft_len), jnp.float32)
    for tap_index in range(tap_count):
        running = running + weights[tap_index] * blocks[
            :, :, tap_index : tap_index + spec_count, :
        ].astype(jnp.float32)
    return running.astype(jnp.bfloat16)


def channelize(filtered, origin):
    _, pol_count, spec_count, fft_len = filtered.shape
    inner = fft_len // RADIX
    twiddle_re, twiddle_im, inner_matrix = dft_tables(fft_len)
    x = filtered.astype(jnp.float32)
    xr = [x[0, :, :, j * inner : (j + 1) * inner] for j in range(RADIX)]
    xi = [x[1, :, :, j * inner : (j + 1) * inner] for j in range(RADIX)]
    ar, ai = xr[0] + xr[2], xi[0] + xi[2]
    br, bi = xr[1] + xr[3], xi[1] + xi[3]
    cr, ci = xr[0] - xr[2], xi[0] - xi[2]
    dr, di = xr[1] - xr[3], xi[1] - xi[3]
    yr = jnp.stack([ar + br, cr + di, ar - br, cr - di], axis=0)
    yi = jnp.stack([ai + bi, ci - dr, ai - bi, ci + dr], axis=0)
    angle = jnp.asarray(2.0 * np.pi * np.outer(np.arange(RADIX), np.arange(inner)) / fft_len, jnp.float32) + origin
    tr, ti, inner_matrix = lax.optimization_barrier(
        (jnp.cos(angle), -jnp.sin(angle), jnp.asarray(inner_matrix, jnp.bfloat16) + origin.astype(jnp.bfloat16))
    )
    tr = tr[:, None, None, :]
    ti = ti[:, None, None, :]
    zr = yr * tr - yi * ti
    zi = yr * ti + yi * tr
    real_rows = jnp.concatenate([zr, zi], axis=-1)
    imag_rows = jnp.concatenate([zi, -zr], axis=-1)
    rows = jnp.stack([real_rows, imag_rows], axis=2).reshape(RADIX * pol_count * 2 * spec_count, 2 * inner)
    product = lax.dot_general(
        inner_matrix,
        rows.astype(jnp.bfloat16),
        (((0,), (1,)), ((), ())),
        preferred_element_type=jnp.float32,
    )
    return product.astype(jnp.bfloat16)


def rotate_parts(ordered):
    half_cols = ordered.shape[2] // 2
    return jnp.concatenate([-ordered[:, :, half_cols:], ordered[:, :, :half_cols]], axis=2)


def correlate_full(ordered, inverse_count):
    rotated = rotate_parts(ordered)
    real_vis = jnp.einsum("cak,cbk->cab", ordered, ordered, preferred_element_type=jnp.float32)
    imag_vis = jnp.einsum("cak,cbk->cab", ordered, rotated, preferred_element_type=jnp.float32)
    return (jnp.stack([real_vis, imag_vis], axis=0) * inverse_count).astype(jnp.bfloat16)


def local(samples, history, coefficients, station_of_slot, station_ok):
    tap_count, fft_len = coefficients.shape
    row_count = samples.shape[1]
    half_count = lax.axis_size("tch")
    block_count = lax.axis_size("blk")
    dest_count = half_count * block_count
    station_count = station_of_slot.shape[0]
    inner = fft_len // RADIX
    kl_count = inner // dest_count
    keep = row_count // half_count
    t = lax.axis_index("tch")
    other = lax.dynamic_slice_in_dim(samples, (1 - t) * keep, keep, axis=1)
    other = other.astype(jnp.float32).reshape(2, keep, -1, fft_len)
    received = lax.ppermute(other, "tch", [(0, 1), (1, 0)])
    own = lax.dynamic_slice_in_dim(samples, t * keep, keep, axis=1)
    own = own.astype(jnp.float32).reshape(2, keep, -1, fft_len)
    before = history.astype(jnp.float32).reshape(2, row_count, -1, fft_len)
    is_first = t == 0
    first = jnp.where(is_first, own, received)
    second = jnp.where(is_first, received, own)
    earlier = lax.dynamic_slice_in_dim(before, t * keep, keep, axis=1)
    extended = jnp.concatenate([earlier, first, second], axis=2).reshape(2, keep, -1)
    spec_total = (extended.shape[2] - (tap_count - 1) * fft_len) // fft_len
    spectra = channelize(filter_bank(extended, coefficients, spec_total), 0.0 * coefficients[0, 0])
    spectra = spectra.reshape(dest_count, kl_count, -1)
    turned = lax.all_to_all(spectra, ("blk", "tch"), split_axis=0, concat_axis=0, tiled=True)
    slot_index = (
        jnp.zeros((station_count,), jnp.int32)
        .at[station_of_slot]
        .set(jnp.arange(station_count, dtype=jnp.int32))
    )
    chan_count = kl_count * RADIX
    input_count = station_count * POLS
    by_source = turned.reshape(station_count, kl_count, RADIX * POLS, 2 * spec_total)
    by_source = jnp.transpose(by_source, (1, 2, 0, 3)).reshape(chan_count, input_count, 2 * spec_total)
    position = jnp.arange(input_count, dtype=jnp.int32)
    wanted = slot_index[position // POLS] + (position % POLS) * station_count
    select = (wanted[:, None] == position[None, :]).astype(turned.dtype)
    select = select * station_ok[position // POLS].astype(turned.dtype)[:, None]
    select = jnp.broadcast_to(select, (chan_count, input_count, input_count))
    ordered = jnp.einsum(
        "cij,cjk->cik", select, by_source, preferred_element_type=jnp.float32
    ).astype(turned.dtype)
    vis = correlate_full(ordered, 1.0 / spec_total)
    return with_layout_constraint(vis, Layout((0, 1, 2, 3)))


def solution(mesh):
    return jax.shard_map(
        local,
        mesh=mesh,
        in_specs=(P("grp", "blk", "tch"), P("grp", "blk", None), P(), P("grp"), P("grp")),
        out_specs=P("grp", ("blk", "tch"), None, None),
        check_vma=False,
    )
```
